128 devices in a mesh: row: 8 (over z, core), col: 16 (over y, x).
Axes of the slice: x: 4, y: 4, z: 4, core: 2. Of those that a mesh axis runs over, the one named last changes fastest.
Arguments:
- psi_val: float32 [64, 128, 128, 128], P(None, 'row', 'col'), may hold values from -6 to 6
- psi_cond: float32 [64, 128, 128, 128], P(None, 'row', 'col'), may hold values from -6 to 6
- eps_val: float32 [64], replicated, may hold values from -12 to -1
- eps_cond: float32 [64], replicated, may hold values from 1 to 12
- val_index: int32 [128], replicated, may hold values from 0 to 63
- cond_index: int32 [128], replicated, may hold values from 0 to 63
- gmap: int32 [8192], replicated, may hold values from 0 to 2097151, as said below
- chi0_in: float32 [2, 8192, 8192], P(None, 'row', 'col'), may hold values from -6 to 6
Outputs:
- chi0_out: float32 [2, 8192, 8192], P(None, 'row', 'col')
The draws below stay inside these ranges and needn't reach their ends.
Inputs may be any that keep to these rules, and one draw needn't show every extreme that they name: gmap holds 8192 distinct entries. Entries g of device block d = g // 64 (d = r * 16 + c) have ky in [r * 16, (r + 1) * 16) and kz in [c * 8, (c + 1) * 8); kx is any.
All inputs are finite; a program needn't handle non-finite values.
Results may differ from the reference program's by a relative error of at most 0.000068.
Values sent between devices are 32-bit elements; how exact they have to be, the bound alone decides.
No kernel may reach another device: no remote copies, remote signals or barrier semaphores. Data moves between devices by JAX's collectives and lax.ppermute only.
A program may use at most 128 MiB of HBM per device.

```python
import math
import jax
import jax.numpy as jnp
from jax import lax

GRID = 128
NG = 8192
NV = 64
NC = 64
P_SIZE = 128
RB = 16
CB = 8
GDEV = 64
MESH_ROWS = 8
MESH_COLS = 16


def pick_block(key, target, block):
    perm = jax.random.permutation(key, block).astype(jnp.int32)
    where_at = jnp.argmax(perm == target)
    first = perm[0]
    perm = perm.at[where_at].set(first)
    perm = perm.at[0].set(target)
    return perm[:GDEV]


def draw_gmap(key, part):
    block = RB * CB * GRID
    count = MESH_ROWS * MESH_COLS
    keys = jax.random.split(key, count)
    device_ids = jnp.arange(count, dtype=jnp.int32)
    targets = jnp.where(device_ids == count - 1, block - 1, 0).astype(jnp.int32)
    picks = jax.vmap(lambda k, t: pick_block(k, t, block))(keys, targets).astype(jnp.int32)
    device = device_ids[:, None]
    row_pos = device // MESH_COLS
    col_pos = device % MESH_COLS
    freq_x = picks % GRID
    rest = picks // GRID
    freq_z = col_pos * CB + rest % CB
    freq_y = row_pos * RB + rest // CB
    return ((freq_x * GRID + freq_y) * GRID + freq_z).reshape(-1).astype(jnp.int32)


def place_ends(entries, rng, smallest, top_value):
    dims = entries.shape
    spot = [jax.random.randint(jax.random.fold_in(rng, axis), (), 0, dims[axis]) for axis in range(len(dims))]
    entries = entries.at[tuple(spot)].set(smallest)
    longest = dims.index(max(dims))
    spot[longest] = (spot[longest] + 1) % dims[longest]
    return entries.at[tuple(spot)].set(top_value)


def levels(stream_key, shape, pieces, smallest, top_value):
    def one(dim, blocks):
        steps = jax.random.uniform(jax.random.fold_in(jax.random.fold_in(stream_key, 6), dim), (blocks,), jnp.float32, smallest / len(pieces), top_value / len(pieces))
        return jnp.repeat(jnp.exp(steps), shape[dim] // blocks).reshape((-1,) + (1,) * (len(shape) - dim - 1))

    loudness = one(*pieces[0])
    for cut in pieces[1:]:
        loudness = loudness * one(*cut)
    return loudness


def scatter_about(key, shape, deviation, most, cuts=(), kind=jnp.bfloat16):
    drawn = jax.random.normal(key, shape, jnp.float32) * deviation
    if len(cuts) > 0:
        drawn = levels(key, shape, cuts, -0.22, 0.18) * drawn
    return jnp.clip(drawn, min=-most, max=most).astype(kind)


def setup_inputs(seed: int = 0) -> dict:
    key_list = jax.random.split(jax.random.key(seed), 9)
    return {
        "psi_val": scatter_about(key_list[0], (NV, GRID, GRID, GRID), 1.0, 6.0, ((1, 8), (2, 16)), jnp.float32),
        "psi_cond": scatter_about(key_list[1], (NC, GRID, GRID, GRID), 1.0, 6.0, ((1, 8), (2, 16)), jnp.float32),
        "eps_val": jnp.clip(jax.random.uniform(key_list[2], (NV,), jnp.float32, -12.0, -1.0), -12.0, -1.0),
        "eps_cond": jnp.clip(jax.random.uniform(key_list[3], (NC,), jnp.float32, 1.0, 12.0), 1.0, 12.0),
        "val_index": place_ends(jax.random.randint(key_list[4], (P_SIZE,), 0, NV), jax.random.fold_in(key_list[4], 1), 0, NV - 1).astype(jnp.int32),
        "cond_index": place_ends(jax.random.randint(key_list[5], (P_SIZE,), 0, NC), jax.random.fold_in(key_list[5], 1), 0, NC - 1).astype(jnp.int32),
        "gmap": draw_gmap(jax.random.fold_in(key_list[8], 71), 0),
        "chi0_in": scatter_about(key_list[7], (2, NG, NG), 1.0, 6.0, ((1, 8), (2, 16)), jnp.float32),
    }


def contract_pairs(left, right):
    return lax.dot_general(left, right, (((0,), (0,)), ((), ())), precision=lax.Precision.HIGHEST, preferred_element_type=jnp.float32)

def reference(psi_val, psi_cond, eps_val, eps_cond, val_index, cond_index, gmap, chi0_in):
    scale = 1.0 / math.sqrt(GRID ** 3)

    def one_pair(pair):
        vband, cband = pair
        rho = psi_val[vband] * psi_cond[cband]
        spec = jnp.fft.fftn(rho).reshape(-1)[gmap]
        return (jnp.real(spec).astype(jnp.float32) * scale, jnp.imag(spec).astype(jnp.float32) * scale)
    m_re, m_im = lax.map(one_pair, (val_index, cond_index))
    weight = -6.0 / (math.sqrt(P_SIZE) * (eps_cond[cond_index] - eps_val[val_index]))
    weight = weight[:, None]
    out_re = chi0_in[0] + contract_pairs(weight * m_re, m_re) + contract_pairs(weight * m_im, m_im)
    out_im = chi0_in[1] + contract_pairs(weight * m_im, m_re) - contract_pairs(weight * m_re, m_im)
    return jnp.stack([out_re, out_im])
```

```python
import math

import jax
import jax.numpy as jnp
from jax import lax
from jax.sharding import PartitionSpec as P

GRID = 128
NG = 8192


HIGH = lax.Precision.HIGHEST


def phase_table(left, right, length):
    phase = left[:, None] * right[None, :] % length
    angle = phase.astype(jnp.float32) * (2.0 * math.pi / length)
    return (jnp.cos(angle), jnp.sin(angle))


def contract_pairs(left, right):
    return lax.dot_general(
        left, right, (((0,), (0,)), ((), ())), precision=HIGH, preferred_element_type=jnp.float32
    )


def on_device(psi_val, psi_cond, eps_val, eps_cond, val_index, cond_index, gmap, chi0_in):
    pairs = val_index.shape[0]
    scale = 1.0 / math.sqrt(GRID**3)
    row_pos = lax.axis_index("row")
    col_pos = lax.axis_index("col")
    mesh_cols = lax.axis_size("col")
    mesh_rows = lax.axis_size("row")
    per_device = NG // (mesh_rows * mesh_cols)
    row_span = GRID // mesh_rows
    col_span = GRID // mesh_cols
    steps = jnp.arange(GRID, dtype=jnp.int32)

    rho = jnp.take(psi_val, val_index, axis=0) * jnp.take(psi_cond, cond_index, axis=0)

    cos_z, sin_z = phase_table(steps, steps, GRID)
    table_z = jnp.stack([cos_z, -sin_z], axis=-1).reshape(GRID, mesh_cols, col_span, 2)
    z_all = jnp.einsum("pxyz,zckt->cpxykt", rho, table_z, precision=HIGH)
    z_mine = lax.all_to_all(z_all, "col", split_axis=0, concat_axis=0, tiled=True)

    cos_y, sin_y = phase_table(steps, steps, GRID)
    table_y = jnp.stack(
        [jnp.stack([cos_y, -sin_y], axis=-1), jnp.stack([sin_y, cos_y], axis=-1)], axis=1
    ).reshape(mesh_cols, col_span, 2, GRID, 2)
    y_all = jnp.einsum("spxykt,syteu->pxeku", z_mine, table_y, precision=HIGH)

    col_map = lax.dynamic_index_in_dim(
        gmap.reshape(mesh_rows, mesh_cols, per_device), col_pos, axis=1, keepdims=False
    ).reshape(-1)
    freq_x = col_map // (GRID * GRID)
    freq_y = col_map // GRID % GRID
    freq_z = col_map % GRID - col_pos * col_span
    pick = freq_y * col_span + freq_z
    flat = y_all.reshape(pairs, row_span, GRID * col_span, 2)
    chosen = jnp.take(flat, pick, axis=2)
    x_glob = row_pos * row_span + jnp.arange(row_span, dtype=jnp.int32)
    cos_x, sin_x = phase_table(x_glob, freq_x, GRID)
    c_re = chosen[..., 0]
    c_im = chosen[..., 1]
    part_re = jnp.sum(c_re * cos_x[None] + c_im * sin_x[None], axis=1)
    part_im = jnp.sum(c_im * cos_x[None] - c_re * sin_x[None], axis=1)
    partial = jnp.stack([part_re, part_im], axis=0) * scale
    own = lax.psum_scatter(partial, "row", scatter_dimension=2, tiled=True)

    rows = lax.all_gather(own, "col", axis=2, tiled=True)
    half = mesh_cols // 2
    send = lax.dynamic_slice_in_dim(rows, (col_pos // half) * half * per_device, half * per_device, 2)
    perm = []
    for src_r in range(mesh_rows):
        for src_c in range(mesh_cols):
            dst_r = src_c % half
            dst_c = 2 * src_r + src_c // half
            perm.append((src_r * mesh_cols + src_c, dst_r * mesh_cols + dst_c))
    cols = lax.ppermute(send, ("row", "col"), perm)

    val_hot = val_index[:, None] == jnp.arange(eps_val.shape[0], dtype=jnp.int32)[None, :]
    cond_hot = cond_index[:, None] == jnp.arange(eps_cond.shape[0], dtype=jnp.int32)[None, :]
    energy_v = jnp.sum(jnp.where(val_hot, eps_val[None, :], 0.0), axis=1)
    energy_c = jnp.sum(jnp.where(cond_hot, eps_cond[None, :], 0.0), axis=1)
    weight = (-6.0 / (math.sqrt(pairs) * (energy_c - energy_v)))[:, None]
    rows_re = rows[0]
    rows_im = rows[1]
    cols_re = cols[0]
    cols_im = cols[1]
    out_re = (
        chi0_in[0]
        + contract_pairs(weight * rows_re, cols_re)
        + contract_pairs(weight * rows_im, cols_im)
    )
    out_im = (
        chi0_in[1]
        + contract_pairs(weight * rows_im, cols_re)
        - contract_pairs(weight * rows_re, cols_im)
    )
    return jnp.stack([out_re, out_im])


def solution(mesh):
    return jax.shard_map(
        on_device,
        mesh=mesh,
        in_specs=(
            P(None, "row", "col", None),
            P(None, "row", "col", None),
            P(),
            P(),
            P(),
            P(),
            P(),
            P(None, "row", "col"),
        ),
        out_specs=P(None, "row", "col"),
        check_vma=False,
    )
```

```python
import math

import jax
import jax.numpy as jnp
from jax import lax
from jax.sharding import PartitionSpec as P

GRID = 128
NG = 8192


HIGH = lax.Precision.HIGHEST


def phase_table(left, right, length):
    phase = left[:, None] * right[None, :] % length
    angle = phase.astype(jnp.float32) * (2.0 * math.pi / length)
    return (jnp.cos(angle), jnp.sin(angle))


def contract_pairs(left, right):
    return lax.dot_general(
        left, right, (((0,), (0,)), ((), ())), precision=HIGH, preferred_element_type=jnp.float32
    )


def on_device(psi_val, psi_cond, eps_val, eps_cond, val_index, cond_index, gmap, chi0_in):
    pairs = val_index.shape[0]
    scale = 1.0 / math.sqrt(GRID**3)
    row_pos = lax.axis_index("row")
    col_pos = lax.axis_index("col")
    mesh_cols = lax.axis_size("col")
    mesh_rows = lax.axis_size("row")
    per_device = NG // (mesh_rows * mesh_cols)
    row_span = GRID // mesh_rows
    col_span = GRID // mesh_cols
    steps = jnp.arange(GRID, dtype=jnp.int32)

    col_map = lax.dynamic_index_in_dim(
        gmap.reshape(mesh_rows, mesh_cols, per_device), col_pos, axis=1, keepdims=False
    ).reshape(-1)
    freq_x = col_map // (GRID * GRID)
    freq_y = col_map // GRID % GRID
    freq_z = col_map % GRID - col_pos * col_span
    pick = freq_y * col_span + freq_z
    x_glob = row_pos * row_span + jnp.arange(row_span, dtype=jnp.int32)
    cos_x, sin_x = phase_table(x_glob, freq_x, GRID)

    cos_z, sin_z = phase_table(steps, steps, GRID)
    table_z = jnp.stack([cos_z, -sin_z], axis=-1).reshape(GRID, mesh_cols, col_span, 2)
    cos_y, sin_y = phase_table(steps, steps, GRID)
    table_y = jnp.stack(
        [jnp.stack([cos_y, -sin_y], axis=-1), jnp.stack([sin_y, cos_y], axis=-1)], axis=1
    ).reshape(mesh_cols, col_span, 2, GRID, 2)

    chunks = 4
    chunk = pairs // chunks
    pieces = []
    for i in range(chunks):
        v_idx = val_index[i * chunk:(i + 1) * chunk]
        c_idx = cond_index[i * chunk:(i + 1) * chunk]
        rho = jnp.take(psi_val, v_idx, axis=0) * jnp.take(psi_cond, c_idx, axis=0)
        z_all = jnp.einsum("pxyz,zckt->cpxykt", rho, table_z, precision=HIGH)
        z_mine = lax.all_to_all(z_all, "col", split_axis=0, concat_axis=0, tiled=True)
        y_all = jnp.einsum("spxykt,syteu->pxeku", z_mine, table_y, precision=HIGH)
        flat = y_all.reshape(chunk, row_span, GRID * col_span, 2)
        chosen = jnp.take(flat, pick, axis=2)
        c_re = chosen[..., 0]
        c_im = chosen[..., 1]
        part_re = jnp.sum(c_re * cos_x[None] + c_im * sin_x[None], axis=1)
        part_im = jnp.sum(c_im * cos_x[None] - c_re * sin_x[None], axis=1)
        pieces.append(jnp.stack([part_re, part_im], axis=0))
    partial = jnp.concatenate(pieces, axis=1) * scale
    spread = partial.reshape(2, pairs, mesh_rows, per_device).transpose(2, 0, 1, 3)
    gathered = lax.all_to_all(spread, "row", split_axis=0, concat_axis=0, tiled=True)
    own = jnp.sum(gathered, axis=0)
    copies = jnp.broadcast_to(own[None], (mesh_cols,) + own.shape)
    row_blocks = lax.all_to_all(copies, "col", split_axis=0, concat_axis=0, tiled=True)
    rows = row_blocks.transpose(1, 2, 0, 3).reshape(2, pairs, mesh_cols * per_device)
    half = mesh_cols // 2
    send = lax.dynamic_slice_in_dim(rows, (col_pos // half) * half * per_device, half * per_device, 2)
    perm = []
    for src_r in range(mesh_rows):
        for src_c in range(mesh_cols):
            dst_r = src_c % half
            dst_c = 2 * src_r + src_c // half
            perm.append((src_r * mesh_cols + src_c, dst_r * mesh_cols + dst_c))
    cols = lax.ppermute(send, ("row", "col"), perm)

    val_hot = val_index[:, None] == jnp.arange(eps_val.shape[0], dtype=jnp.int32)[None, :]
    cond_hot = cond_index[:, None] == jnp.arange(eps_cond.shape[0], dtype=jnp.int32)[None, :]
    energy_v = jnp.sum(jnp.where(val_hot, eps_val[None, :], 0.0), axis=1)
    energy_c = jnp.sum(jnp.where(cond_hot, eps_cond[None, :], 0.0), axis=1)
    weight = (-6.0 / (math.sqrt(pairs) * (energy_c - energy_v)))[:, None]
    rows_re = rows[0]
    rows_im = rows[1]
    cols_re = cols[0]
    cols_im = cols[1]
    out_re = (
        chi0_in[0]
        + contract_pairs(weight * rows_re, cols_re)
        + contract_pairs(weight * rows_im, cols_im)
    )
    out_im = (
        chi0_in[1]
        + contract_pairs(weight * rows_im, cols_re)
        - contract_pairs(weight * rows_re, cols_im)
    )
    return jnp.stack([out_re, out_im])


def solution(mesh):
    return jax.shard_map(
        on_device,
        mesh=mesh,
        in_specs=(
            P(None, "row", "col", None),
            P(None, "row", "col", None),
            P(),
            P(),
            P(),
            P(),
            P(),
            P(None, "row", "col"),
        ),
        out_specs=P(None, "row", "col"),
        check_vma=False,
    )
```

```python
import math

import jax
import jax.numpy as jnp
from jax import lax
from jax.sharding import PartitionSpec as P

GRID = 128
NG = 8192


HIGH = lax.Precision.HIGHEST


def phase_table(left, right, length):
    phase = left[:, None] * right[None, :] % length
    angle = phase.astype(jnp.float32) * (2.0 * math.pi / length)
    return (jnp.cos(angle), jnp.sin(angle))


def contract_pairs(left, right):
    return lax.dot_general(
        left, right, (((0,), (0,)), ((), ())), precision=HIGH, preferred_element_type=jnp.float32
    )


def on_device(psi_val, psi_cond, eps_val, eps_cond, val_index, cond_index, gmap, chi0_in):
    pairs = val_index.shape[0]
    scale = 1.0 / math.sqrt(GRID**3)
    row_pos = lax.axis_index("row")
    col_pos = lax.axis_index("col")
    mesh_cols = lax.axis_size("col")
    mesh_rows = lax.axis_size("row")
    per_device = NG // (mesh_rows * mesh_cols)
    row_span = GRID // mesh_rows
    col_span = GRID // mesh_cols
    steps = jnp.arange(GRID, dtype=jnp.int32)

    col_map = lax.dynamic_index_in_dim(
        gmap.reshape(mesh_rows, mesh_cols, per_device), col_pos, axis=1, keepdims=False
    ).reshape(-1)
    freq_x = col_map // (GRID * GRID)
    freq_y = col_map // GRID % GRID
    freq_z = col_map % GRID - col_pos * col_span
    pick = freq_y * col_span + freq_z
    x_glob = row_pos * row_span + jnp.arange(row_span, dtype=jnp.int32)
    cos_x, sin_x = phase_table(x_glob, freq_x, GRID)

    cos_z, sin_z = phase_table(steps, steps, GRID)
    table_z = jnp.stack([cos_z, -sin_z], axis=-1).reshape(GRID, mesh_cols, col_span, 2)
    cos_y, sin_y = phase_table(steps, steps, GRID)
    table_y = jnp.stack(
        [jnp.stack([cos_y, -sin_y], axis=-1), jnp.stack([sin_y, cos_y], axis=-1)], axis=1
    ).reshape(mesh_cols, col_span, 2, GRID, 2)

    rho = jnp.take(psi_val, val_index, axis=0) * jnp.take(psi_cond, cond_index, axis=0)
    chunks = 4
    chunk = row_span // chunks
    partial = None
    for i in range(chunks):
        rho_part = rho[:, i * chunk:(i + 1) * chunk]
        z_all = jnp.einsum("pxyz,zckt->cpxykt", rho_part, table_z, precision=HIGH)
        z_mine = lax.all_to_all(z_all, "col", split_axis=0, concat_axis=0, tiled=True)
        y_all = jnp.einsum("spxykt,syteu->pxeku", z_mine, table_y, precision=HIGH)
        flat = y_all.reshape(pairs, chunk, GRID * col_span, 2)
        chosen = jnp.take(flat, pick, axis=2)
        c_re = chosen[..., 0]
        c_im = chosen[..., 1]
        cx = cos_x[i * chunk:(i + 1) * chunk]
        sx = sin_x[i * chunk:(i + 1) * chunk]
        part_re = jnp.sum(c_re * cx[None] + c_im * sx[None], axis=1)
        part_im = jnp.sum(c_im * cx[None] - c_re * sx[None], axis=1)
        piece = jnp.stack([part_re, part_im], axis=0)
        partial = piece if partial is None else partial + piece
    partial = partial * scale
    spread = partial.reshape(2, pairs, mesh_rows, per_device).transpose(2, 0, 1, 3)
    gathered = lax.all_to_all(spread, "row", split_axis=0, concat_axis=0, tiled=True)
    own = jnp.sum(gathered, axis=0)
    copies = jnp.broadcast_to(own[None], (mesh_cols,) + own.shape)
    row_blocks = lax.all_to_all(copies, "col", split_axis=0, concat_axis=0, tiled=True)
    rows = row_blocks.transpose(1, 2, 0, 3).reshape(2, pairs, mesh_cols * per_device)
    half = mesh_cols // 2
    send = lax.dynamic_slice_in_dim(rows, (col_pos // half) * half * per_device, half * per_device, 2)
    perm = []
    for src_r in range(mesh_rows):
        for src_c in range(mesh_cols):
            dst_r = src_c % half
            dst_c = 2 * src_r + src_c // half
            perm.append((src_r * mesh_cols + src_c, dst_r * mesh_cols + dst_c))
    cols = lax.ppermute(send, ("row", "col"), perm)

    val_hot = val_index[:, None] == jnp.arange(eps_val.shape[0], dtype=jnp.int32)[None, :]
    cond_hot = cond_index[:, None] == jnp.arange(eps_cond.shape[0], dtype=jnp.int32)[None, :]
    energy_v = jnp.sum(jnp.where(val_hot, eps_val[None, :], 0.0), axis=1)
    energy_c = jnp.sum(jnp.where(cond_hot, eps_cond[None, :], 0.0), axis=1)
    weight = (-6.0 / (math.sqrt(pairs) * (energy_c - energy_v)))[:, None]
    rows_re = rows[0]
    rows_im = rows[1]
    cols_re = cols[0]
    cols_im = cols[1]
    out_re = (
        chi0_in[0]
        + contract_pairs(weight * rows_re, cols_re)
        + contract_pairs(weight * rows_im, cols_im)
    )
    out_im = (
        chi0_in[1]
        + contract_pairs(weight * rows_im, cols_re)
        - contract_pairs(weight * rows_re, cols_im)
    )
    return jnp.stack([out_re, out_im])


def solution(mesh):
    return jax.shard_map(
        on_device,
        mesh=mesh,
        in_specs=(
            P(None, "row", "col", None),
            P(None, "row", "col", None),
            P(),
            P(),
            P(),
            P(),
            P(),
            P(None, "row", "col"),
        ),
        out_specs=P(None, "row", "col"),
        check_vma=False,
    )
```

```python
import math

import jax
import numpy as np
import jax.numpy as jnp
from jax import lax
from jax.sharding import PartitionSpec as P

GRID = 128
NG = 8192


HIGH = lax.Precision.HIGHEST


def phase_table(left, right, length):
    phase = left[:, None] * right[None, :] % length
    angle = phase.astype(jnp.float32) * (2.0 * math.pi / length)
    return (jnp.cos(angle), jnp.sin(angle))


def contract_pairs(left, right):
    return lax.dot_general(
        left, right, (((0,), (0,)), ((), ())), precision=HIGH, preferred_element_type=jnp.float32
    )


def on_device(psi_val, psi_cond, eps_val, eps_cond, val_index, cond_index, gmap, chi0_in):
    pairs = val_index.shape[0]
    scale = 1.0 / math.sqrt(GRID**3)
    row_pos = lax.axis_index("row")
    col_pos = lax.axis_index("col")
    mesh_cols = lax.axis_size("col")
    mesh_rows = lax.axis_size("row")
    per_device = NG // (mesh_rows * mesh_cols)
    row_span = GRID // mesh_rows
    col_span = GRID // mesh_cols
    steps = jnp.arange(GRID, dtype=jnp.int32)

    halves = 2
    half_pairs = pairs // halves
    mirror = mesh_cols - 1 - col_pos
    low = jnp.minimum(col_pos, mirror)
    side = col_pos // (mesh_cols // 2)
    span_z = col_span + 1
    by_block = gmap.reshape(mesh_rows, mesh_cols, per_device)
    direct = lax.dynamic_index_in_dim(by_block, low, axis=1, keepdims=False)
    mirrored = lax.dynamic_index_in_dim(by_block, mesh_cols - 1 - low, axis=1, keepdims=False)
    both = jnp.stack([direct, mirrored], axis=1).reshape(-1)
    flip = (jnp.arange(both.shape[0], dtype=jnp.int32) // per_device) % 2
    freq_x = both // (GRID * GRID)
    freq_y = both // GRID % GRID
    freq_z = both % GRID
    freq_x = jnp.where(flip == 1, (GRID - freq_x) % GRID, freq_x)
    freq_y = jnp.where(flip == 1, (GRID - freq_y) % GRID, freq_y)
    freq_z = jnp.where(flip == 1, (GRID - freq_z) % GRID, freq_z) - low * col_span
    sign = jnp.where(flip == 1, -1.0, 1.0).astype(jnp.float32)
    pick = freq_y * span_z + freq_z
    x_glob = row_pos * row_span + jnp.arange(row_span, dtype=jnp.int32)
    cos_x, sin_x = phase_table(x_glob, freq_x, GRID)

    kz_set = (jnp.arange(mesh_cols // 2, dtype=jnp.int32)[:, None] * col_span
              + jnp.arange(span_z, dtype=jnp.int32)[None, :]).reshape(-1)
    cos_z, sin_z = phase_table(steps, kz_set, GRID)
    table_z = jnp.stack([cos_z, -sin_z], axis=-1).reshape(GRID, mesh_cols // 2, span_z, 2)
    table_z = jnp.stack([table_z, table_z[:, ::-1]], axis=0)
    cos_y, sin_y = phase_table(steps, steps, GRID)
    table_y = jnp.stack(
        [jnp.stack([cos_y, -sin_y], axis=-1), jnp.stack([sin_y, cos_y], axis=-1)], axis=1
    ).reshape(mesh_cols, col_span, 2, GRID, 2)

    chunks = 4
    chunk = row_span // chunks
    partial = None
    for i in range(chunks):
        xs = slice(i * chunk, (i + 1) * chunk)
        rho = jnp.take(psi_val[:, xs], val_index, axis=0) * jnp.take(psi_cond[:, xs], cond_index, axis=0)
        rho = rho.reshape((halves, half_pairs) + rho.shape[1:])
        z_all = jnp.einsum("hpxyz,hzcjt->hcpxyjt", rho, table_z, precision=HIGH)
        z_all = z_all.reshape((mesh_cols,) + z_all.shape[2:])
        z_mine = lax.all_to_all(z_all, "col", split_axis=0, concat_axis=0, tiled=True)
        y_all = jnp.einsum("spxyjt,syteu->pxeju", z_mine, table_y, precision=HIGH)
        flat = y_all.reshape(half_pairs, chunk, GRID * span_z, 2)
        chosen = jnp.take(flat, pick, axis=2)
        c_re = chosen[..., 0]
        c_im = chosen[..., 1]
        cx = cos_x[xs]
        sx = sin_x[xs]
        part_re = jnp.sum(c_re * cx[None] + c_im * sx[None], axis=1)
        part_im = jnp.sum(c_im * cx[None] - c_re * sx[None], axis=1)
        piece = jnp.stack([part_re, part_im], axis=0)
        partial = piece if partial is None else partial + piece
    partial = partial * jnp.stack([jnp.ones_like(sign), sign])[:, None, :] * scale
    block = 2 * per_device
    spread = partial.reshape(2, half_pairs, mesh_rows, block).transpose(2, 0, 1, 3)
    gathered = lax.all_to_all(spread, "row", split_axis=0, concat_axis=0, tiled=True)
    own = jnp.sum(gathered, axis=0).reshape(2, half_pairs, 2, per_device)
    copies = jnp.broadcast_to(own[None], (mesh_cols,) + own.shape)
    got = lax.all_to_all(copies, "col", split_axis=0, concat_axis=0, tiled=True)
    parts = []
    for h in range(halves):
        src = []
        slot = []
        for c in range(mesh_cols):
            lower = c < mesh_cols // 2
            if h == 0:
                src.append(c if lower else mesh_cols - 1 - c)
            else:
                src.append(mesh_cols - 1 - c if lower else c)
            slot.append(0 if lower else 1)
        sel = got[np.array(src), :, :, np.array(slot), :]
        parts.append(sel.transpose(1, 2, 0, 3).reshape(2, half_pairs, mesh_cols * per_device))
    rows = jnp.concatenate(parts, axis=1)
    half = mesh_cols // 2
    send = lax.dynamic_slice_in_dim(rows, (col_pos // half) * half * per_device, half * per_device, 2)
    perm = []
    for src_r in range(mesh_rows):
        for src_c in range(mesh_cols):
            dst_r = src_c % half
            dst_c = 2 * src_r + src_c // half
            perm.append((src_r * mesh_cols + src_c, dst_r * mesh_cols + dst_c))
    cols = lax.ppermute(send, ("row", "col"), perm)

    val_hot = val_index[:, None] == jnp.arange(eps_val.shape[0], dtype=jnp.int32)[None, :]
    cond_hot = cond_index[:, None] == jnp.arange(eps_cond.shape[0], dtype=jnp.int32)[None, :]
    energy_v = jnp.sum(jnp.where(val_hot, eps_val[None, :], 0.0), axis=1)
    energy_c = jnp.sum(jnp.where(cond_hot, eps_cond[None, :], 0.0), axis=1)
    weight = (-6.0 / (math.sqrt(pairs) * (energy_c - energy_v)))[:, None]
    rows_re = rows[0]
    rows_im = rows[1]
    cols_re = cols[0]
    cols_im = cols[1]
    out_re = (
        chi0_in[0]
        + contract_pairs(weight * rows_re, cols_re)
        + contract_pairs(weight * rows_im, cols_im)
    )
    out_im = (
        chi0_in[1]
        + contract_pairs(weight * rows_im, cols_re)
        - contract_pairs(weight * rows_re, cols_im)
    )
    return jnp.stack([out_re, out_im])


def solution(mesh):
    return jax.shard_map(
        on_device,
        mesh=mesh,
        in_specs=(
            P(None, "row", "col", None),
            P(None, "row", "col", None),
            P(),
            P(),
            P(),
            P(),
            P(),
            P(None, "row", "col"),
        ),
        out_specs=P(None, "row", "col"),
        check_vma=False,
    )
```

```python
import math

import jax
import numpy as np
import jax.numpy as jnp
from jax import lax
from jax.sharding import PartitionSpec as P

GRID = 128
NG = 8192


HIGH = lax.Precision.HIGHEST


def phase_table(left, right, length):
    phase = left[:, None] * right[None, :] % length
    angle = phase.astype(jnp.float32) * (2.0 * math.pi / length)
    return (jnp.cos(angle), jnp.sin(angle))


def contract_pairs(left, right):
    return lax.dot_general(
        left, right, (((0,), (0,)), ((), ())), precision=HIGH, preferred_element_type=jnp.float32
    )


def on_device(psi_val, psi_cond, eps_val, eps_cond, val_index, cond_index, gmap, chi0_in):
    pairs = val_index.shape[0]
    scale = 1.0 / math.sqrt(GRID**3)
    row_pos = lax.axis_index("row")
    col_pos = lax.axis_index("col")
    mesh_cols = lax.axis_size("col")
    mesh_rows = lax.axis_size("row")
    per_device = NG // (mesh_rows * mesh_cols)
    row_span = GRID // mesh_rows
    col_span = GRID // mesh_cols
    steps = jnp.arange(GRID, dtype=jnp.int32)

    mirror = mesh_cols - 1 - col_pos
    low = jnp.minimum(col_pos, mirror)
    side = col_pos // (mesh_cols // 2)
    span_z = col_span + 1
    x_half = row_span // 2
    by_block = gmap.reshape(mesh_rows, mesh_cols, per_device)
    direct = lax.dynamic_index_in_dim(by_block, low, axis=1, keepdims=False)
    mirrored = lax.dynamic_index_in_dim(by_block, mesh_cols - 1 - low, axis=1, keepdims=False)
    both = jnp.stack([direct, mirrored], axis=1).reshape(-1)
    flip = (jnp.arange(both.shape[0], dtype=jnp.int32) // per_device) % 2
    freq_x = both // (GRID * GRID)
    freq_y = both // GRID % GRID
    freq_z = both % GRID
    freq_x = jnp.where(flip == 1, (GRID - freq_x) % GRID, freq_x)
    freq_y = jnp.where(flip == 1, (GRID - freq_y) % GRID, freq_y)
    freq_z = jnp.where(flip == 1, (GRID - freq_z) % GRID, freq_z) - low * col_span
    sign = jnp.where(flip == 1, -1.0, 1.0).astype(jnp.float32)
    pick = freq_y * span_z + freq_z
    x_glob = row_pos * row_span + side * x_half + jnp.arange(x_half, dtype=jnp.int32)
    cos_x, sin_x = phase_table(x_glob, freq_x, GRID)

    kz_set = (jnp.arange(mesh_cols // 2, dtype=jnp.int32)[:, None] * col_span
              + jnp.arange(span_z, dtype=jnp.int32)[None, :]).reshape(-1)
    cos_z, sin_z = phase_table(steps, kz_set, GRID)
    table_z = jnp.stack([cos_z, -sin_z], axis=-1).reshape(GRID, mesh_cols // 2, span_z, 2)
    table_z = jnp.stack([table_z, table_z[:, ::-1]], axis=0)
    cos_y, sin_y = phase_table(steps, steps, GRID)
    table_y = jnp.stack(
        [jnp.stack([cos_y, -sin_y], axis=-1), jnp.stack([sin_y, cos_y], axis=-1)], axis=1
    ).reshape(mesh_cols, col_span, 2, GRID, 2)

    chunks = 4
    chunk = x_half // chunks
    partial = None
    for i in range(chunks):
        lo = slice(i * chunk, (i + 1) * chunk)
        hi = slice(x_half + i * chunk, x_half + (i + 1) * chunk)
        band_v = jnp.stack([psi_val[:, lo], psi_val[:, hi]], axis=1)
        band_c = jnp.stack([psi_cond[:, lo], psi_cond[:, hi]], axis=1)
        rho = jnp.take(band_v, val_index, axis=0) * jnp.take(band_c, cond_index, axis=0)
        z_all = jnp.einsum("phxyz,hzcjt->hcpxyjt", rho, table_z, precision=HIGH)
        z_all = z_all.reshape((mesh_cols,) + z_all.shape[2:])
        z_mine = lax.all_to_all(z_all, "col", split_axis=0, concat_axis=0, tiled=True)
        y_all = jnp.einsum("spxyjt,syteu->pxeju", z_mine, table_y, precision=HIGH)
        flat = y_all.reshape(pairs, chunk, GRID * span_z, 2)
        chosen = jnp.take(flat, pick, axis=2)
        c_re = chosen[..., 0]
        c_im = chosen[..., 1]
        cx = cos_x[lo]
        sx = sin_x[lo]
        part_re = jnp.sum(c_re * cx[None] + c_im * sx[None], axis=1)
        part_im = jnp.sum(c_im * cx[None] - c_re * sx[None], axis=1)
        piece = jnp.stack([part_re, part_im], axis=0)
        partial = piece if partial is None else partial + piece
    partial = partial * jnp.stack([jnp.ones_like(sign), sign])[:, None, :] * scale
    block = 2 * per_device
    spread = partial.reshape(2, pairs, mesh_rows, block).transpose(2, 0, 1, 3)
    gathered = lax.all_to_all(spread, "row", split_axis=0, concat_axis=0, tiled=True)
    both_blocks = jnp.sum(gathered, axis=0).reshape(2, pairs, 2, per_device)
    mine = lax.dynamic_index_in_dim(both_blocks, side, axis=2, keepdims=False)
    theirs = lax.dynamic_index_in_dim(both_blocks, 1 - side, axis=2, keepdims=False)
    partner = lax.ppermute(theirs, "col", [(c, mesh_cols - 1 - c) for c in range(mesh_cols)])
    own = mine + partner
    copies = jnp.broadcast_to(own[None], (mesh_cols,) + own.shape)
    row_blocks = lax.all_to_all(copies, "col", split_axis=0, concat_axis=0, tiled=True)
    rows = row_blocks.transpose(1, 2, 0, 3).reshape(2, pairs, mesh_cols * per_device)
    half = mesh_cols // 2
    send = lax.dynamic_slice_in_dim(rows, (col_pos // half) * half * per_device, half * per_device, 2)
    perm = []
    for src_r in range(mesh_rows):
        for src_c in range(mesh_cols):
            dst_r = src_c % half
            dst_c = 2 * src_r + src_c // half
            perm.append((src_r * mesh_cols + src_c, dst_r * mesh_cols + dst_c))
    cols = lax.ppermute(send, ("row", "col"), perm)

    val_hot = val_index[:, None] == jnp.arange(eps_val.shape[0], dtype=jnp.int32)[None, :]
    cond_hot = cond_index[:, None] == jnp.arange(eps_cond.shape[0], dtype=jnp.int32)[None, :]
    energy_v = jnp.sum(jnp.where(val_hot, eps_val[None, :], 0.0), axis=1)
    energy_c = jnp.sum(jnp.where(cond_hot, eps_cond[None, :], 0.0), axis=1)
    weight = (-6.0 / (math.sqrt(pairs) * (energy_c - energy_v)))[:, None]
    rows_re = rows[0]
    rows_im = rows[1]
    cols_re = cols[0]
    cols_im = cols[1]
    out_re = (
        chi0_in[0]
        + contract_pairs(weight * rows_re, cols_re)
        + contract_pairs(weight * rows_im, cols_im)
    )
    out_im = (
        chi0_in[1]
        + contract_pairs(weight * rows_im, cols_re)
        - contract_pairs(weight * rows_re, cols_im)
    )
    return jnp.stack([out_re, out_im])


def solution(mesh):
    return jax.shard_map(
        on_device,
        mesh=mesh,
        in_specs=(
            P(None, "row", "col", None),
            P(None, "row", "col", None),
            P(),
            P(),
            P(),
            P(),
            P(),
            P(None, "row", "col"),
        ),
        out_specs=P(None, "row", "col"),
        check_vma=False,
    )
```

```python
import math

import jax
import numpy as np
import jax.numpy as jnp
from jax import lax
from jax.sharding import PartitionSpec as P

GRID = 128
NG = 8192


HIGH = lax.Precision.HIGHEST


def phase_table(left, right, length):
    phase = left[:, None] * right[None, :] % length
    angle = phase.astype(jnp.float32) * (2.0 * math.pi / length)
    return (jnp.cos(angle), jnp.sin(angle))


def contract_pairs(left, right):
    return lax.dot_general(
        left, right, (((1,), (1,)), ((), ())), precision=HIGH, preferred_element_type=jnp.float32
    )


def on_device(psi_val, psi_cond, eps_val, eps_cond, val_index, cond_index, gmap, chi0_in):
    pairs = val_index.shape[0]
    scale = 1.0 / math.sqrt(GRID**3)
    row_pos = lax.axis_index("row")
    col_pos = lax.axis_index("col")
    mesh_cols = lax.axis_size("col")
    mesh_rows = lax.axis_size("row")
    per_device = NG // (mesh_rows * mesh_cols)
    row_span = GRID // mesh_rows
    col_span = GRID // mesh_cols
    steps = jnp.arange(GRID, dtype=jnp.int32)

    mirror = mesh_cols - 1 - col_pos
    low = jnp.minimum(col_pos, mirror)
    side = col_pos // (mesh_cols // 2)
    span_z = col_span + 1
    x_half = row_span // 2
    by_block = gmap.reshape(mesh_rows, mesh_cols, per_device)
    direct = lax.dynamic_index_in_dim(by_block, low, axis=1, keepdims=False)
    mirrored = lax.dynamic_index_in_dim(by_block, mesh_cols - 1 - low, axis=1, keepdims=False)
    both = jnp.stack([direct, mirrored], axis=1).reshape(-1)
    flip = (jnp.arange(both.shape[0], dtype=jnp.int32) // per_device) % 2
    freq_x = both // (GRID * GRID)
    freq_y = both // GRID % GRID
    freq_z = both % GRID
    freq_x = jnp.where(flip == 1, (GRID - freq_x) % GRID, freq_x)
    freq_y = jnp.where(flip == 1, (GRID - freq_y) % GRID, freq_y)
    freq_z = jnp.where(flip == 1, (GRID - freq_z) % GRID, freq_z) - low * col_span
    sign = jnp.where(flip == 1, -1.0, 1.0).astype(jnp.float32)
    pick = freq_y * span_z + freq_z
    x_glob = row_pos * row_span + side * x_half + jnp.arange(x_half, dtype=jnp.int32)
    cos_x, sin_x = phase_table(x_glob, freq_x, GRID)

    kz_set = (jnp.arange(mesh_cols // 2, dtype=jnp.int32)[:, None] * col_span
              + jnp.arange(span_z, dtype=jnp.int32)[None, :]).reshape(-1)
    cos_z, sin_z = phase_table(steps, kz_set, GRID)
    table_z = jnp.stack([cos_z, -sin_z], axis=-1).reshape(GRID, mesh_cols // 2, span_z, 2)
    table_z = jnp.stack([table_z, table_z[:, ::-1]], axis=0)
    cos_y, sin_y = phase_table(steps, steps, GRID)
    table_y = jnp.stack(
        [jnp.stack([cos_y, -sin_y], axis=-1), jnp.stack([sin_y, cos_y], axis=-1)], axis=1
    ).reshape(mesh_cols, col_span, 2, GRID, 2)

    chunks = 4
    chunk = x_half // chunks
    partial = None
    for i in range(chunks):
        lo = slice(i * chunk, (i + 1) * chunk)
        hi = slice(x_half + i * chunk, x_half + (i + 1) * chunk)
        band_v = jnp.stack([psi_val[:, lo], psi_val[:, hi]], axis=1)
        band_c = jnp.stack([psi_cond[:, lo], psi_cond[:, hi]], axis=1)
        rho = jnp.take(band_v, val_index, axis=0) * jnp.take(band_c, cond_index, axis=0)
        z_all = jnp.einsum("phxyz,hzcjt->hcpxyjt", rho, table_z, precision=HIGH)
        z_all = z_all.reshape((mesh_cols,) + z_all.shape[2:])
        z_mine = lax.all_to_all(z_all, "col", split_axis=0, concat_axis=0, tiled=True)
        y_all = jnp.einsum("spxyjt,syteu->ejuxp", z_mine, table_y, precision=HIGH)
        flat = y_all.reshape(GRID * span_z, 2, chunk, pairs)
        chosen = jnp.take(flat, pick, axis=0)
        c_re = chosen[:, 0]
        c_im = chosen[:, 1]
        cx = cos_x[lo].T[:, :, None]
        sx = sin_x[lo].T[:, :, None]
        part_re = jnp.sum(c_re * cx + c_im * sx, axis=1)
        part_im = jnp.sum(c_im * cx - c_re * sx, axis=1)
        piece = jnp.stack([part_re, part_im], axis=1)
        partial = piece if partial is None else partial + piece
    partial = partial * jnp.stack([jnp.ones_like(sign), sign], axis=1)[:, :, None] * scale
    block = 2 * per_device
    spread = partial.reshape(mesh_rows, block, 2, pairs)
    gathered = lax.all_to_all(spread, "row", split_axis=0, concat_axis=0, tiled=True)
    both_blocks = jnp.sum(gathered, axis=0).reshape(2, per_device, 2, pairs)
    mine = lax.dynamic_index_in_dim(both_blocks, side, axis=0, keepdims=False)
    theirs = lax.dynamic_index_in_dim(both_blocks, 1 - side, axis=0, keepdims=False)
    partner = lax.ppermute(theirs, "col", [(c, mesh_cols - 1 - c) for c in range(mesh_cols)])
    own = mine + partner
    copies = jnp.broadcast_to(own[None], (mesh_cols,) + own.shape)
    row_blocks = lax.all_to_all(copies, "col", split_axis=0, concat_axis=0, tiled=True)
    rows = row_blocks.reshape(mesh_cols * per_device, 2, pairs)
    half = mesh_cols // 2
    send = lax.dynamic_slice_in_dim(rows, (col_pos // half) * half * per_device, half * per_device, 0)
    perm = []
    for src_r in range(mesh_rows):
        for src_c in range(mesh_cols):
            dst_r = src_c % half
            dst_c = 2 * src_r + src_c // half
            perm.append((src_r * mesh_cols + src_c, dst_r * mesh_cols + dst_c))
    cols = lax.ppermute(send, ("row", "col"), perm)

    val_hot = val_index[:, None] == jnp.arange(eps_val.shape[0], dtype=jnp.int32)[None, :]
    cond_hot = cond_index[:, None] == jnp.arange(eps_cond.shape[0], dtype=jnp.int32)[None, :]
    energy_v = jnp.sum(jnp.where(val_hot, eps_val[None, :], 0.0), axis=1)
    energy_c = jnp.sum(jnp.where(cond_hot, eps_cond[None, :], 0.0), axis=1)
    weight = (-6.0 / (math.sqrt(pairs) * (energy_c - energy_v)))[None, :]
    rows_re = rows[:, 0]
    rows_im = rows[:, 1]
    cols_re = cols[:, 0]
    cols_im = cols[:, 1]
    out_re = (
        chi0_in[0]
        + contract_pairs(weight * rows_re, cols_re)
        + contract_pairs(weight * rows_im, cols_im)
    )
    out_im = (
        chi0_in[1]
        + contract_pairs(weight * rows_im, cols_re)
        - contract_pairs(weight * rows_re, cols_im)
    )
    return jnp.stack([out_re, out_im])


def solution(mesh):
    return jax.shard_map(
        on_device,
        mesh=mesh,
        in_specs=(
            P(None, "row", "col", None),
            P(None, "row", "col", None),
            P(),
            P(),
            P(),
            P(),
            P(),
            P(None, "row", "col"),
        ),
        out_specs=P(None, "row", "col"),
        check_vma=False,
    )
```

```python
import math

import jax
import numpy as np
import jax.numpy as jnp
from jax import lax
from jax.sharding import PartitionSpec as P

GRID = 128
NG = 8192


HIGH = lax.Precision.HIGHEST


def phase_table(left, right, length):
    phase = left[:, None] * right[None, :] % length
    angle = phase.astype(jnp.float32) * (2.0 * math.pi / length)
    return (jnp.cos(angle), jnp.sin(angle))


def contract_pairs(left, right):
    return lax.dot_general(
        left, right, (((1,), (1,)), ((), ())), precision=HIGH, preferred_element_type=jnp.float32
    )


def on_device(psi_val, psi_cond, eps_val, eps_cond, val_index, cond_index, gmap, chi0_in):
    pairs = val_index.shape[0]
    scale = 1.0 / math.sqrt(GRID**3)
    row_pos = lax.axis_index("row")
    col_pos = lax.axis_index("col")
    mesh_cols = lax.axis_size("col")
    mesh_rows = lax.axis_size("row")
    per_device = NG // (mesh_rows * mesh_cols)
    row_span = GRID // mesh_rows
    col_span = GRID // mesh_cols
    steps = jnp.arange(GRID, dtype=jnp.int32)

    mirror = mesh_cols - 1 - col_pos
    low = jnp.minimum(col_pos, mirror)
    side = col_pos // (mesh_cols // 2)
    span_z = col_span + 1
    x_half = row_span // 2
    by_block = gmap.reshape(mesh_rows, mesh_cols, per_device)
    direct = lax.dynamic_index_in_dim(by_block, low, axis=1, keepdims=False)
    mirrored = lax.dynamic_index_in_dim(by_block, mesh_cols - 1 - low, axis=1, keepdims=False)
    both = jnp.stack([direct, mirrored], axis=1).reshape(-1)
    flip = (jnp.arange(both.shape[0], dtype=jnp.int32) // per_device) % 2
    freq_x = both // (GRID * GRID)
    freq_y = both // GRID % GRID
    freq_z = both % GRID
    freq_x = jnp.where(flip == 1, (GRID - freq_x) % GRID, freq_x)
    freq_y = jnp.where(flip == 1, (GRID - freq_y) % GRID, freq_y)
    freq_z = jnp.where(flip == 1, (GRID - freq_z) % GRID, freq_z) - low * col_span
    sign = jnp.where(flip == 1, -1.0, 1.0).astype(jnp.float32)
    pick = freq_y * span_z + freq_z
    x_glob = row_pos * row_span + side * x_half + jnp.arange(x_half, dtype=jnp.int32)
    cos_x, sin_x = phase_table(x_glob, freq_x, GRID)

    kz_set = (jnp.arange(mesh_cols // 2, dtype=jnp.int32)[:, None] * col_span
              + jnp.arange(span_z, dtype=jnp.int32)[None, :]).reshape(-1)
    cos_z, sin_z = phase_table(steps, kz_set, GRID)
    table_z = jnp.stack([cos_z, -sin_z], axis=-1).reshape(GRID, mesh_cols // 2, span_z, 2)
    table_z = jnp.stack([table_z, table_z[:, ::-1]], axis=0)
    cos_y, sin_y = phase_table(steps, steps, GRID)
    table_y = jnp.stack(
        [jnp.stack([cos_y, -sin_y], axis=-1), jnp.stack([sin_y, cos_y], axis=-1)], axis=1
    ).reshape(mesh_cols, col_span, 2, GRID, 2)

    chunks = 4
    chunk = x_half // chunks
    pieces = []
    for i in range(chunks):
        lo = slice(i * chunk, (i + 1) * chunk)
        hi = slice(x_half + i * chunk, x_half + (i + 1) * chunk)
        band_v = jnp.stack([psi_val[:, lo], psi_val[:, hi]], axis=1)
        band_c = jnp.stack([psi_cond[:, lo], psi_cond[:, hi]], axis=1)
        rho = jnp.take(band_v, val_index, axis=0) * jnp.take(band_c, cond_index, axis=0)
        z_all = jnp.einsum("phxyz,hzcjt->hcpxyjt", rho, table_z, precision=HIGH)
        z_all = z_all.reshape((mesh_cols,) + z_all.shape[2:])
        if i >= 2:
            z_all, pieces[i - 2] = lax.optimization_barrier((z_all, pieces[i - 2]))
        z_mine = lax.all_to_all(z_all, "col", split_axis=0, concat_axis=0, tiled=True)
        y_all = jnp.einsum("spxyjt,syteu->ejuxp", z_mine, table_y, precision=HIGH)
        flat = y_all.reshape(GRID * span_z, 2, chunk, pairs)
        chosen = jnp.take(flat, pick, axis=0)
        c_re = chosen[:, 0]
        c_im = chosen[:, 1]
        cx = cos_x[lo].T[:, :, None]
        sx = sin_x[lo].T[:, :, None]
        part_re = jnp.sum(c_re * cx + c_im * sx, axis=1)
        part_im = jnp.sum(c_im * cx - c_re * sx, axis=1)
        pieces.append(jnp.stack([part_re, part_im], axis=1))
    partial = pieces[0]
    for piece in pieces[1:]:
        partial = partial + piece
    partial = partial * jnp.stack([jnp.ones_like(sign), sign], axis=1)[:, :, None] * scale
    block = 2 * per_device
    spread = partial.reshape(mesh_rows, block, 2, pairs)
    gathered = lax.all_to_all(spread, "row", split_axis=0, concat_axis=0, tiled=True)
    both_blocks = jnp.sum(gathered, axis=0).reshape(2, per_device, 2, pairs)
    mine = lax.dynamic_index_in_dim(both_blocks, side, axis=0, keepdims=False)
    theirs = lax.dynamic_index_in_dim(both_blocks, 1 - side, axis=0, keepdims=False)
    partner = lax.ppermute(theirs, "col", [(c, mesh_cols - 1 - c) for c in range(mesh_cols)])
    own = mine + partner
    copies = jnp.broadcast_to(own[None], (mesh_cols,) + own.shape)
    row_blocks = lax.all_to_all(copies, "col", split_axis=0, concat_axis=0, tiled=True)
    rows = row_blocks.reshape(mesh_cols * per_device, 2, pairs)
    half = mesh_cols // 2
    send = lax.dynamic_slice_in_dim(rows, (col_pos // half) * half * per_device, half * per_device, 0)
    perm = []
    for src_r in range(mesh_rows):
        for src_c in range(mesh_cols):
            dst_r = src_c % half
            dst_c = 2 * src_r + src_c // half
            perm.append((src_r * mesh_cols + src_c, dst_r * mesh_cols + dst_c))
    cols = lax.ppermute(send, ("row", "col"), perm)

    val_hot = val_index[:, None] == jnp.arange(eps_val.shape[0], dtype=jnp.int32)[None, :]
    cond_hot = cond_index[:, None] == jnp.arange(eps_cond.shape[0], dtype=jnp.int32)[None, :]
    energy_v = jnp.sum(jnp.where(val_hot, eps_val[None, :], 0.0), axis=1)
    energy_c = jnp.sum(jnp.where(cond_hot, eps_cond[None, :], 0.0), axis=1)
    weight = (-6.0 / (math.sqrt(pairs) * (energy_c - energy_v)))[None, :]
    rows_re = rows[:, 0]
    rows_im = rows[:, 1]
    cols_re = cols[:, 0]
    cols_im = cols[:, 1]
    out_re = (
        chi0_in[0]
        + contract_pairs(weight * rows_re, cols_re)
        + contract_pairs(weight * rows_im, cols_im)
    )
    out_im = (
        chi0_in[1]
        + contract_pairs(weight * rows_im, cols_re)
        - contract_pairs(weight * rows_re, cols_im)
    )
    return jnp.stack([out_re, out_im])


def solution(mesh):
    return jax.shard_map(
        on_device,
        mesh=mesh,
        in_specs=(
            P(None, "row", "col", None),
            P(None, "row", "col", None),
            P(),
            P(),
            P(),
            P(),
            P(),
            P(None, "row", "col"),
        ),
        out_specs=P(None, "row", "col"),
        check_vma=False,
    )
```

```python
import math

import jax
import numpy as np
import jax.numpy as jnp
from jax import lax
from jax.sharding import PartitionSpec as P

GRID = 128
NG = 8192


HIGH = lax.Precision.HIGHEST


def phase_table(left, right, length):
    phase = left[:, None] * right[None, :] % length
    angle = phase.astype(jnp.float32) * (2.0 * math.pi / length)
    return (jnp.cos(angle), jnp.sin(angle))


def contract_pairs(left, right):
    return lax.dot_general(
        left, right, (((1,), (1,)), ((), ())), precision=HIGH, preferred_element_type=jnp.float32
    )


def on_device(psi_val, psi_cond, eps_val, eps_cond, val_index, cond_index, gmap, chi0_in):
    pairs = val_index.shape[0]
    scale = 1.0 / math.sqrt(GRID**3)
    row_pos = lax.axis_index("row")
    col_pos = lax.axis_index("col")
    mesh_cols = lax.axis_size("col")
    mesh_rows = lax.axis_size("row")
    per_device = NG // (mesh_rows * mesh_cols)
    row_span = GRID // mesh_rows
    col_span = GRID // mesh_cols
    steps = jnp.arange(GRID, dtype=jnp.int32)

    mirror = mesh_cols - 1 - col_pos
    low = jnp.minimum(col_pos, mirror)
    side = col_pos // (mesh_cols // 2)
    span_z = col_span + 1
    x_half = row_span // 2
    by_block = gmap.reshape(mesh_rows, mesh_cols, per_device)
    direct = lax.dynamic_index_in_dim(by_block, low, axis=1, keepdims=False)
    mirrored = lax.dynamic_index_in_dim(by_block, mesh_cols - 1 - low, axis=1, keepdims=False)
    both = jnp.stack([direct, mirrored], axis=1).reshape(-1)
    flip = (jnp.arange(both.shape[0], dtype=jnp.int32) // per_device) % 2
    freq_x = both // (GRID * GRID)
    freq_y = both // GRID % GRID
    freq_z = both % GRID
    freq_x = jnp.where(flip == 1, (GRID - freq_x) % GRID, freq_x)
    freq_y = jnp.where(flip == 1, (GRID - freq_y) % GRID, freq_y)
    freq_z = jnp.where(flip == 1, (GRID - freq_z) % GRID, freq_z) - low * col_span
    sign = jnp.where(flip == 1, -1.0, 1.0).astype(jnp.float32)
    pick = freq_y * span_z + freq_z
    x_glob = row_pos * row_span + side * x_half + jnp.arange(x_half, dtype=jnp.int32)
    cos_x, sin_x = phase_table(x_glob, freq_x, GRID)

    kz_set = (jnp.arange(mesh_cols // 2, dtype=jnp.int32)[:, None] * col_span
              + jnp.arange(span_z, dtype=jnp.int32)[None, :]).reshape(-1)
    cos_z, sin_z = phase_table(steps, kz_set, GRID)
    table_z = jnp.stack([cos_z, -sin_z], axis=-1).reshape(GRID, mesh_cols // 2, span_z, 2)
    table_z = jnp.stack([table_z, table_z[:, ::-1]], axis=0)
    cos_y, sin_y = phase_table(steps, steps, GRID)
    table_y = jnp.stack(
        [jnp.stack([cos_y, -sin_y], axis=-1), jnp.stack([sin_y, cos_y], axis=-1)], axis=1
    ).reshape(mesh_cols, col_span, 2, GRID, 2)

    chunks = 2
    chunk = x_half // chunks
    pieces = []
    for i in range(chunks):
        lo = slice(i * chunk, (i + 1) * chunk)
        hi = slice(x_half + i * chunk, x_half + (i + 1) * chunk)
        band_v = jnp.stack([psi_val[:, lo], psi_val[:, hi]], axis=1)
        band_c = jnp.stack([psi_cond[:, lo], psi_cond[:, hi]], axis=1)
        rho = jnp.take(band_v, val_index, axis=0) * jnp.take(band_c, cond_index, axis=0)
        z_all = jnp.einsum("phxyz,hzcjt->hcpxyjt", rho, table_z, precision=HIGH)
        z_all = z_all.reshape((mesh_cols,) + z_all.shape[2:])
        if i >= 2:
            z_all, pieces[i - 2] = lax.optimization_barrier((z_all, pieces[i - 2]))
        z_mine = lax.all_to_all(z_all, "col", split_axis=0, concat_axis=0, tiled=True)
        y_all = jnp.einsum("spxyjt,syteu->ejuxp", z_mine, table_y, precision=HIGH)
        flat = y_all.reshape(GRID * span_z, 2, chunk, pairs)
        chosen = jnp.take(flat, pick, axis=0)
        c_re = chosen[:, 0]
        c_im = chosen[:, 1]
        cx = cos_x[lo].T[:, :, None]
        sx = sin_x[lo].T[:, :, None]
        part_re = jnp.sum(c_re * cx + c_im * sx, axis=1)
        part_im = jnp.sum(c_im * cx - c_re * sx, axis=1)
        pieces.append(jnp.stack([part_re, part_im], axis=1))
    partial = pieces[0]
    for piece in pieces[1:]:
        partial = partial + piece
    partial = partial * jnp.stack([jnp.ones_like(sign), sign], axis=1)[:, :, None] * scale
    block = 2 * per_device
    spread = partial.reshape(mesh_rows, block, 2, pairs)
    gathered = lax.all_to_all(spread, "row", split_axis=0, concat_axis=0, tiled=True)
    both_blocks = jnp.sum(gathered, axis=0).reshape(2, per_device, 2, pairs)
    mine = lax.dynamic_index_in_dim(both_blocks, side, axis=0, keepdims=False)
    theirs = lax.dynamic_index_in_dim(both_blocks, 1 - side, axis=0, keepdims=False)
    partner = lax.ppermute(theirs, "col", [(c, mesh_cols - 1 - c) for c in range(mesh_cols)])
    own = mine + partner
    copies = jnp.broadcast_to(own[None], (mesh_cols,) + own.shape)
    row_blocks = lax.all_to_all(copies, "col", split_axis=0, concat_axis=0, tiled=True)
    rows = row_blocks.reshape(mesh_cols * per_device, 2, pairs)
    half = mesh_cols // 2
    send = lax.dynamic_slice_in_dim(rows, (col_pos // half) * half * per_device, half * per_device, 0)
    perm = []
    for src_r in range(mesh_rows):
        for src_c in range(mesh_cols):
            dst_r = src_c % half
            dst_c = 2 * src_r + src_c // half
            perm.append((src_r * mesh_cols + src_c, dst_r * mesh_cols + dst_c))
    cols = lax.ppermute(send, ("row", "col"), perm)

    val_hot = val_index[:, None] == jnp.arange(eps_val.shape[0], dtype=jnp.int32)[None, :]
    cond_hot = cond_index[:, None] == jnp.arange(eps_cond.shape[0], dtype=jnp.int32)[None, :]
    energy_v = jnp.sum(jnp.where(val_hot, eps_val[None, :], 0.0), axis=1)
    energy_c = jnp.sum(jnp.where(cond_hot, eps_cond[None, :], 0.0), axis=1)
    weight = (-6.0 / (math.sqrt(pairs) * (energy_c - energy_v)))[None, :]
    rows_re = rows[:, 0]
    rows_im = rows[:, 1]
    cols_re = cols[:, 0]
    cols_im = cols[:, 1]
    out_re = (
        chi0_in[0]
        + contract_pairs(weight * rows_re, cols_re)
        + contract_pairs(weight * rows_im, cols_im)
    )
    out_im = (
        chi0_in[1]
        + contract_pairs(weight * rows_im, cols_re)
        - contract_pairs(weight * rows_re, cols_im)
    )
    return jnp.stack([out_re, out_im])


def solution(mesh):
    return jax.shard_map(
        on_device,
        mesh=mesh,
        in_specs=(
            P(None, "row", "col", None),
            P(None, "row", "col", None),
            P(),
            P(),
            P(),
            P(),
            P(),
            P(None, "row", "col"),
        ),
        out_specs=P(None, "row", "col"),
        check_vma=False,
    )
```

```python
import math

import jax
import numpy as np
import jax.numpy as jnp
from jax import lax
from jax.sharding import PartitionSpec as P

GRID = 128
NG = 8192


HIGH = lax.Precision.HIGHEST


def phase_table(left, right, length):
    phase = left[:, None] * right[None, :] % length
    angle = phase.astype(jnp.float32) * (2.0 * math.pi / length)
    return (jnp.cos(angle), jnp.sin(angle))


def contract_pairs(left, right):
    return lax.dot_general(
        left, right, (((1,), (1,)), ((), ())), precision=HIGH, preferred_element_type=jnp.float32
    )


def on_device(psi_val, psi_cond, eps_val, eps_cond, val_index, cond_index, gmap, chi0_in):
    pairs = val_index.shape[0]
    scale = 1.0 / math.sqrt(GRID**3)
    row_pos = lax.axis_index("row")
    col_pos = lax.axis_index("col")
    mesh_cols = lax.axis_size("col")
    mesh_rows = lax.axis_size("row")
    per_device = NG // (mesh_rows * mesh_cols)
    row_span = GRID // mesh_rows
    col_span = GRID // mesh_cols
    steps = jnp.arange(GRID, dtype=jnp.int32)

    mirror = mesh_cols - 1 - col_pos
    low = jnp.minimum(col_pos, mirror)
    side = col_pos // (mesh_cols // 2)
    span_z = col_span + 1
    x_half = row_span // 2
    by_block = gmap.reshape(mesh_rows, mesh_cols, per_device)
    direct = lax.dynamic_index_in_dim(by_block, low, axis=1, keepdims=False)
    mirrored = lax.dynamic_index_in_dim(by_block, mesh_cols - 1 - low, axis=1, keepdims=False)
    both = jnp.stack([direct, mirrored], axis=1).reshape(-1)
    flip = (jnp.arange(both.shape[0], dtype=jnp.int32) // per_device) % 2
    freq_x = both // (GRID * GRID)
    freq_y = both // GRID % GRID
    freq_z = both % GRID
    freq_x = jnp.where(flip == 1, (GRID - freq_x) % GRID, freq_x)
    freq_y = jnp.where(flip == 1, (GRID - freq_y) % GRID, freq_y)
    freq_z = jnp.where(flip == 1, (GRID - freq_z) % GRID, freq_z) - low * col_span
    sign = jnp.where(flip == 1, -1.0, 1.0).astype(jnp.float32)
    pick = freq_y * span_z + freq_z
    x_glob = row_pos * row_span + side * x_half + jnp.arange(x_half, dtype=jnp.int32)
    cos_x, sin_x = phase_table(x_glob, freq_x, GRID)

    kz_set = (jnp.arange(mesh_cols // 2, dtype=jnp.int32)[:, None] * col_span
              + jnp.arange(span_z, dtype=jnp.int32)[None, :]).reshape(-1)
    cos_z, sin_z = phase_table(steps, kz_set, GRID)
    table_z = jnp.stack([cos_z, -sin_z], axis=-1).reshape(GRID, mesh_cols // 2, span_z, 2)
    table_z = jnp.stack([table_z, table_z[:, ::-1]], axis=0)
    cos_y, sin_y = phase_table(steps, steps, GRID)
    table_y = jnp.stack(
        [jnp.stack([cos_y, -sin_y], axis=-1), jnp.stack([sin_y, cos_y], axis=-1)], axis=1
    ).reshape(mesh_cols, col_span, 2, GRID, 2)

    chunks = 2
    chunk = x_half // chunks
    pieces = []
    for i in range(chunks):
        lo = slice(i * chunk, (i + 1) * chunk)
        hi = slice(x_half + i * chunk, x_half + (i + 1) * chunk)
        band_v = jnp.stack([psi_val[:, lo], psi_val[:, hi]], axis=1)
        band_c = jnp.stack([psi_cond[:, lo], psi_cond[:, hi]], axis=1)
        rho = jnp.take(band_v, val_index, axis=0) * jnp.take(band_c, cond_index, axis=0)
        z_all = jnp.einsum("phxyz,hzcjt->hcpxyjt", rho, table_z, precision=HIGH)
        z_all = z_all.reshape((mesh_cols,) + z_all.shape[2:])
        z_mine = lax.all_to_all(z_all, "col", split_axis=0, concat_axis=0, tiled=True)
        if i >= 1:
            z_mine, pieces[i - 1] = lax.optimization_barrier((z_mine, pieces[i - 1]))
        y_all = jnp.einsum("spxyjt,syteu->ejuxp", z_mine, table_y, precision=HIGH)
        flat = y_all.reshape(GRID * span_z, 2, chunk, pairs)
        chosen = jnp.take(flat, pick, axis=0)
        c_re = chosen[:, 0]
        c_im = chosen[:, 1]
        cx = cos_x[lo].T[:, :, None]
        sx = sin_x[lo].T[:, :, None]
        part_re = jnp.sum(c_re * cx + c_im * sx, axis=1)
        part_im = jnp.sum(c_im * cx - c_re * sx, axis=1)
        pieces.append(jnp.stack([part_re, part_im], axis=1))
    partial = pieces[0]
    for piece in pieces[1:]:
        partial = partial + piece
    partial = partial * jnp.stack([jnp.ones_like(sign), sign], axis=1)[:, :, None] * scale
    block = 2 * per_device
    spread = partial.reshape(mesh_rows, block, 2, pairs)
    gathered = lax.all_to_all(spread, "row", split_axis=0, concat_axis=0, tiled=True)
    both_blocks = jnp.sum(gathered, axis=0).reshape(2, per_device, 2, pairs)
    mine = lax.dynamic_index_in_dim(both_blocks, side, axis=0, keepdims=False)
    theirs = lax.dynamic_index_in_dim(both_blocks, 1 - side, axis=0, keepdims=False)
    partner = lax.ppermute(theirs, "col", [(c, mesh_cols - 1 - c) for c in range(mesh_cols)])
    own = mine + partner
    copies = jnp.broadcast_to(own[None], (mesh_cols,) + own.shape)
    row_blocks = lax.all_to_all(copies, "col", split_axis=0, concat_axis=0, tiled=True)
    rows = row_blocks.reshape(mesh_cols * per_device, 2, pairs)
    half = mesh_cols // 2
    send = lax.dynamic_slice_in_dim(rows, (col_pos // half) * half * per_device, half * per_device, 0)
    perm = []
    for src_r in range(mesh_rows):
        for src_c in range(mesh_cols):
            dst_r = src_c % half
            dst_c = 2 * src_r + src_c // half
            perm.append((src_r * mesh_cols + src_c, dst_r * mesh_cols + dst_c))
    cols = lax.ppermute(send, ("row", "col"), perm)

    val_hot = val_index[:, None] == jnp.arange(eps_val.shape[0], dtype=jnp.int32)[None, :]
    cond_hot = cond_index[:, None] == jnp.arange(eps_cond.shape[0], dtype=jnp.int32)[None, :]
    energy_v = jnp.sum(jnp.where(val_hot, eps_val[None, :], 0.0), axis=1)
    energy_c = jnp.sum(jnp.where(cond_hot, eps_cond[None, :], 0.0), axis=1)
    weight = (-6.0 / (math.sqrt(pairs) * (energy_c - energy_v)))[None, :]
    rows_re = rows[:, 0]
    rows_im = rows[:, 1]
    cols_re = cols[:, 0]
    cols_im = cols[:, 1]
    out_re = (
        chi0_in[0]
        + contract_pairs(weight * rows_re, cols_re)
        + contract_pairs(weight * rows_im, cols_im)
    )
    out_im = (
        chi0_in[1]
        + contract_pairs(weight * rows_im, cols_re)
        - contract_pairs(weight * rows_re, cols_im)
    )
    return jnp.stack([out_re, out_im])


def solution(mesh):
    return jax.shard_map(
        on_device,
        mesh=mesh,
        in_specs=(
            P(None, "row", "col", None),
            P(None, "row", "col", None),
            P(),
            P(),
            P(),
            P(),
            P(),
            P(None, "row", "col"),
        ),
        out_specs=P(None, "row", "col"),
        check_vma=False,
    )
```

```python
import math

import jax
import numpy as np
import jax.numpy as jnp
from jax import lax
from jax.sharding import PartitionSpec as P

GRID = 128
NG = 8192


HIGH = lax.Precision.HIGHEST


def phase_table(left, right, length):
    phase = left[:, None] * right[None, :] % length
    angle = phase.astype(jnp.float32) * (2.0 * math.pi / length)
    return (jnp.cos(angle), jnp.sin(angle))


def contract_pairs(left, right):
    return lax.dot_general(
        left, right, (((1,), (1,)), ((), ())), precision=HIGH, preferred_element_type=jnp.float32
    )


def on_device(psi_val, psi_cond, eps_val, eps_cond, val_index, cond_index, gmap, chi0_in):
    pairs = val_index.shape[0]
    scale = 1.0 / math.sqrt(GRID**3)
    row_pos = lax.axis_index("row")
    col_pos = lax.axis_index("col")
    mesh_cols = lax.axis_size("col")
    mesh_rows = lax.axis_size("row")
    per_device = NG // (mesh_rows * mesh_cols)
    row_span = GRID // mesh_rows
    col_span = GRID // mesh_cols
    steps = jnp.arange(GRID, dtype=jnp.int32)

    mirror = mesh_cols - 1 - col_pos
    low = jnp.minimum(col_pos, mirror)
    side = col_pos // (mesh_cols // 2)
    span_z = col_span + 1
    x_half = row_span // 2
    by_block = gmap.reshape(mesh_rows, mesh_cols, per_device)
    direct = lax.dynamic_index_in_dim(by_block, low, axis=1, keepdims=False)
    mirrored = lax.dynamic_index_in_dim(by_block, mesh_cols - 1 - low, axis=1, keepdims=False)
    both = jnp.stack([direct, mirrored], axis=1).reshape(-1)
    flip = (jnp.arange(both.shape[0], dtype=jnp.int32) // per_device) % 2
    freq_x = both // (GRID * GRID)
    freq_y = both // GRID % GRID
    freq_z = both % GRID
    freq_x = jnp.where(flip == 1, (GRID - freq_x) % GRID, freq_x)
    freq_y = jnp.where(flip == 1, (GRID - freq_y) % GRID, freq_y)
    freq_z = jnp.where(flip == 1, (GRID - freq_z) % GRID, freq_z) - low * col_span
    sign = jnp.where(flip == 1, -1.0, 1.0).astype(jnp.float32)
    pick = freq_y * span_z + freq_z
    x_glob = row_pos * row_span + side * x_half + jnp.arange(x_half, dtype=jnp.int32)
    cos_x, sin_x = phase_table(x_glob, freq_x, GRID)

    kz_set = (jnp.arange(mesh_cols // 2, dtype=jnp.int32)[:, None] * col_span
              + jnp.arange(span_z, dtype=jnp.int32)[None, :]).reshape(-1)
    cos_z, sin_z = phase_table(steps, kz_set, GRID)
    table_z = jnp.stack([cos_z, -sin_z], axis=-1).reshape(GRID, mesh_cols // 2, span_z, 2)
    table_z = jnp.stack([table_z, table_z[:, ::-1]], axis=0)
    cos_y, sin_y = phase_table(steps, steps, GRID)
    table_y = jnp.stack(
        [jnp.stack([cos_y, -sin_y], axis=-1), jnp.stack([sin_y, cos_y], axis=-1)], axis=1
    ).reshape(mesh_cols, col_span, 2, GRID, 2)

    chunks = 2
    chunk = x_half // chunks
    pieces = []
    for i in range(chunks):
        lo = slice(i * chunk, (i + 1) * chunk)
        hi = slice(x_half + i * chunk, x_half + (i + 1) * chunk)
        band_v = jnp.stack([psi_val[:, lo], psi_val[:, hi]], axis=1)
        band_c = jnp.stack([psi_cond[:, lo], psi_cond[:, hi]], axis=1)
        rho = jnp.take(band_v, val_index, axis=0) * jnp.take(band_c, cond_index, axis=0)
        z_all = jnp.einsum("phxyz,hzcjt->hcpxyjt", rho, table_z, precision=HIGH)
        z_all = z_all.reshape((mesh_cols,) + z_all.shape[2:])
        z_mine = lax.all_to_all(z_all, "col", split_axis=0, concat_axis=0, tiled=True)
        if i >= 1:
            z_mine, pieces[i - 1] = lax.optimization_barrier((z_mine, pieces[i - 1]))
        y_all = jnp.einsum("spxyjt,syteu->ejuxp", z_mine, table_y, precision=HIGH)
        flat = y_all.reshape(GRID * span_z, 2, chunk, pairs)
        chosen = jnp.take(flat, pick, axis=0)
        c_re = chosen[:, 0]
        c_im = chosen[:, 1]
        cx = cos_x[lo].T[:, :, None]
        sx = sin_x[lo].T[:, :, None]
        part_re = jnp.sum(c_re * cx + c_im * sx, axis=1)
        part_im = jnp.sum(c_im * cx - c_re * sx, axis=1)
        pieces.append(jnp.stack([part_re, part_im], axis=1))
    partial = pieces[0]
    for piece in pieces[1:]:
        partial = partial + piece
    partial = partial * jnp.stack([jnp.ones_like(sign), sign], axis=1)[:, :, None] * scale
    block = 2 * per_device
    spread = partial.reshape(mesh_rows, block, 2, pairs)
    summed = lax.dynamic_index_in_dim(spread, row_pos, axis=0, keepdims=False)
    for k in range(1, mesh_rows):
        out = lax.dynamic_index_in_dim(spread, (row_pos + k) % mesh_rows, axis=0, keepdims=False)
        summed = summed + lax.ppermute(out, "row", [(r, (r + k) % mesh_rows) for r in range(mesh_rows)])
    both_blocks = summed.reshape(2, per_device, 2, pairs)
    mine = lax.dynamic_index_in_dim(both_blocks, side, axis=0, keepdims=False)
    theirs = lax.dynamic_index_in_dim(both_blocks, 1 - side, axis=0, keepdims=False)
    partner = lax.ppermute(theirs, "col", [(c, mesh_cols - 1 - c) for c in range(mesh_cols)])
    own = mine + partner
    arrived = [own]
    for k in range(1, mesh_cols):
        arrived.append(lax.ppermute(own, "col", [(c, (c + k) % mesh_cols) for c in range(mesh_cols)]))
    order = (col_pos - jnp.arange(mesh_cols, dtype=jnp.int32)) % mesh_cols
    rows = jnp.take(jnp.stack(arrived), order, axis=0).reshape(mesh_cols * per_device, 2, pairs)
    half = mesh_cols // 2
    send = lax.dynamic_slice_in_dim(rows, (col_pos // half) * half * per_device, half * per_device, 0)
    perm = []
    for src_r in range(mesh_rows):
        for src_c in range(mesh_cols):
            dst_r = src_c % half
            dst_c = 2 * src_r + src_c // half
            perm.append((src_r * mesh_cols + src_c, dst_r * mesh_cols + dst_c))
    cols = lax.ppermute(send, ("row", "col"), perm)

    val_hot = val_index[:, None] == jnp.arange(eps_val.shape[0], dtype=jnp.int32)[None, :]
    cond_hot = cond_index[:, None] == jnp.arange(eps_cond.shape[0], dtype=jnp.int32)[None, :]
    energy_v = jnp.sum(jnp.where(val_hot, eps_val[None, :], 0.0), axis=1)
    energy_c = jnp.sum(jnp.where(cond_hot, eps_cond[None, :], 0.0), axis=1)
    weight = (-6.0 / (math.sqrt(pairs) * (energy_c - energy_v)))[None, :]
    rows_re = rows[:, 0]
    rows_im = rows[:, 1]
    cols_re = cols[:, 0]
    cols_im = cols[:, 1]
    out_re = (
        chi0_in[0]
        + contract_pairs(weight * rows_re, cols_re)
        + contract_pairs(weight * rows_im, cols_im)
    )
    out_im = (
        chi0_in[1]
        + contract_pairs(weight * rows_im, cols_re)
        - contract_pairs(weight * rows_re, cols_im)
    )
    return jnp.stack([out_re, out_im])


def solution(mesh):
    return jax.shard_map(
        on_device,
        mesh=mesh,
        in_specs=(
            P(None, "row", "col", None),
            P(None, "row", "col", None),
            P(),
            P(),
            P(),
            P(),
            P(),
            P(None, "row", "col"),
        ),
        out_specs=P(None, "row", "col"),
        check_vma=False,
    )
```

```python
import math

import jax
import numpy as np
import jax.numpy as jnp
from jax import lax
from jax.sharding import PartitionSpec as P

GRID = 128
NG = 8192


HIGH = lax.Precision.HIGHEST


def phase_table(left, right, length):
    phase = left[:, None] * right[None, :] % length
    angle = phase.astype(jnp.float32) * (2.0 * math.pi / length)
    return (jnp.cos(angle), jnp.sin(angle))


def contract_pairs(left, right):
    return lax.dot_general(
        left, right, (((1,), (1,)), ((), ())), precision=HIGH, preferred_element_type=jnp.float32
    )


def on_device(psi_val, psi_cond, eps_val, eps_cond, val_index, cond_index, gmap, chi0_in):
    pairs = val_index.shape[0]
    scale = 1.0 / math.sqrt(GRID**3)
    row_pos = lax.axis_index("row")
    col_pos = lax.axis_index("col")
    mesh_cols = lax.axis_size("col")
    mesh_rows = lax.axis_size("row")
    per_device = NG // (mesh_rows * mesh_cols)
    row_span = GRID // mesh_rows
    col_span = GRID // mesh_cols
    steps = jnp.arange(GRID, dtype=jnp.int32)

    mirror = mesh_cols - 1 - col_pos
    low = jnp.minimum(col_pos, mirror)
    side = col_pos // (mesh_cols // 2)
    span_z = col_span + 1
    x_half = row_span // 2
    by_block = gmap.reshape(mesh_rows, mesh_cols, per_device)
    direct = lax.dynamic_index_in_dim(by_block, low, axis=1, keepdims=False)
    mirrored = lax.dynamic_index_in_dim(by_block, mesh_cols - 1 - low, axis=1, keepdims=False)
    both = jnp.stack([direct, mirrored], axis=1).reshape(-1)
    flip = (jnp.arange(both.shape[0], dtype=jnp.int32) // per_device) % 2
    freq_x = both // (GRID * GRID)
    freq_y = both // GRID % GRID
    freq_z = both % GRID
    freq_x = jnp.where(flip == 1, (GRID - freq_x) % GRID, freq_x)
    freq_y = jnp.where(flip == 1, (GRID - freq_y) % GRID, freq_y)
    freq_z = jnp.where(flip == 1, (GRID - freq_z) % GRID, freq_z) - low * col_span
    sign = jnp.where(flip == 1, -1.0, 1.0).astype(jnp.float32)
    pick = freq_y * span_z + freq_z
    x_glob = row_pos * row_span + side * x_half + jnp.arange(x_half, dtype=jnp.int32)
    cos_x, sin_x = phase_table(x_glob, freq_x, GRID)

    kz_set = (jnp.arange(mesh_cols // 2, dtype=jnp.int32)[:, None] * col_span
              + jnp.arange(span_z, dtype=jnp.int32)[None, :]).reshape(-1)
    cos_z, sin_z = phase_table(steps, kz_set, GRID)
    table_z = jnp.stack([cos_z, -sin_z], axis=-1).reshape(GRID, mesh_cols // 2, span_z, 2)
    table_z = jnp.stack([table_z, table_z[:, ::-1]], axis=0)
    cos_y, sin_y = phase_table(steps, steps, GRID)
    table_y = jnp.stack(
        [jnp.stack([cos_y, -sin_y], axis=-1), jnp.stack([sin_y, cos_y], axis=-1)], axis=1
    ).reshape(mesh_cols, col_span, 2, GRID, 2)

    sizes = [x_half // 4, x_half // 2, x_half // 4]
    pieces = []
    for i, chunk in enumerate(sizes):
        start = sum(sizes[:i])
        lo = slice(start, start + chunk)
        hi = slice(x_half + start, x_half + start + chunk)
        band_v = jnp.stack([psi_val[:, lo], psi_val[:, hi]], axis=1)
        band_c = jnp.stack([psi_cond[:, lo], psi_cond[:, hi]], axis=1)
        rho = jnp.take(band_v, val_index, axis=0) * jnp.take(band_c, cond_index, axis=0)
        z_all = jnp.einsum("phxyz,hzcjt->hcpxyjt", rho, table_z, precision=HIGH)
        z_all = z_all.reshape((mesh_cols,) + z_all.shape[2:])
        z_mine = lax.all_to_all(z_all, "col", split_axis=0, concat_axis=0, tiled=True)
        if i >= 1:
            z_mine, pieces[i - 1] = lax.optimization_barrier((z_mine, pieces[i - 1]))
        y_all = jnp.einsum("spxyjt,syteu->ejuxp", z_mine, table_y, precision=HIGH)
        flat = y_all.reshape(GRID * span_z, 2, chunk, pairs)
        chosen = jnp.take(flat, pick, axis=0)
        c_re = chosen[:, 0]
        c_im = chosen[:, 1]
        cx = cos_x[lo].T[:, :, None]
        sx = sin_x[lo].T[:, :, None]
        part_re = jnp.sum(c_re * cx + c_im * sx, axis=1)
        part_im = jnp.sum(c_im * cx - c_re * sx, axis=1)
        pieces.append(jnp.stack([part_re, part_im], axis=1))
    partial = pieces[0]
    for piece in pieces[1:]:
        partial = partial + piece
    partial = partial * jnp.stack([jnp.ones_like(sign), sign], axis=1)[:, :, None] * scale
    block = 2 * per_device
    spread = partial.reshape(mesh_rows, block, 2, pairs)
    gathered = lax.all_to_all(spread, "row", split_axis=0, concat_axis=0, tiled=True)
    both_blocks = jnp.sum(gathered, axis=0).reshape(2, per_device, 2, pairs)
    mine = lax.dynamic_index_in_dim(both_blocks, side, axis=0, keepdims=False)
    theirs = lax.dynamic_index_in_dim(both_blocks, 1 - side, axis=0, keepdims=False)
    partner = lax.ppermute(theirs, "col", [(c, mesh_cols - 1 - c) for c in range(mesh_cols)])
    own = mine + partner
    copies = jnp.broadcast_to(own[None], (mesh_cols,) + own.shape)
    row_blocks = lax.all_to_all(copies, "col", split_axis=0, concat_axis=0, tiled=True)
    rows = row_blocks.reshape(mesh_cols * per_device, 2, pairs)
    half = mesh_cols // 2
    send = lax.dynamic_slice_in_dim(rows, (col_pos // half) * half * per_device, half * per_device, 0)
    perm = []
    for src_r in range(mesh_rows):
        for src_c in range(mesh_cols):
            dst_r = src_c % half
            dst_c = 2 * src_r + src_c // half
            perm.append((src_r * mesh_cols + src_c, dst_r * mesh_cols + dst_c))
    cols = lax.ppermute(send, ("row", "col"), perm)

    val_hot = val_index[:, None] == jnp.arange(eps_val.shape[0], dtype=jnp.int32)[None, :]
    cond_hot = cond_index[:, None] == jnp.arange(eps_cond.shape[0], dtype=jnp.int32)[None, :]
    energy_v = jnp.sum(jnp.where(val_hot, eps_val[None, :], 0.0), axis=1)
    energy_c = jnp.sum(jnp.where(cond_hot, eps_cond[None, :], 0.0), axis=1)
    weight = (-6.0 / (math.sqrt(pairs) * (energy_c - energy_v)))[None, :]
    rows_re = rows[:, 0]
    rows_im = rows[:, 1]
    cols_re = cols[:, 0]
    cols_im = cols[:, 1]
    out_re = (
        chi0_in[0]
        + contract_pairs(weight * rows_re, cols_re)
        + contract_pairs(weight * rows_im, cols_im)
    )
    out_im = (
        chi0_in[1]
        + contract_pairs(weight * rows_im, cols_re)
        - contract_pairs(weight * rows_re, cols_im)
    )
    return jnp.stack([out_re, out_im])


def solution(mesh):
    return jax.shard_map(
        on_device,
        mesh=mesh,
        in_specs=(
            P(None, "row", "col", None),
            P(None, "row", "col", None),
            P(),
            P(),
            P(),
            P(),
            P(),
            P(None, "row", "col"),
        ),
        out_specs=P(None, "row", "col"),
        check_vma=False,
    )
```

```python
import math

import jax
import numpy as np
import jax.numpy as jnp
from jax import lax
from jax.sharding import PartitionSpec as P

GRID = 128
NG = 8192


HIGH = lax.Precision.HIGHEST


def phase_table(left, right, length):
    phase = left[:, None] * right[None, :] % length
    angle = phase.astype(jnp.float32) * (2.0 * math.pi / length)
    return (jnp.cos(angle), jnp.sin(angle))


def contract_pairs(left, right):
    return lax.dot_general(
        left, right, (((1,), (1,)), ((), ())), precision=HIGH, preferred_element_type=jnp.float32
    )


def on_device(psi_val, psi_cond, eps_val, eps_cond, val_index, cond_index, gmap, chi0_in):
    pairs = val_index.shape[0]
    scale = 1.0 / math.sqrt(GRID**3)
    row_pos = lax.axis_index("row")
    col_pos = lax.axis_index("col")
    mesh_cols = lax.axis_size("col")
    mesh_rows = lax.axis_size("row")
    per_device = NG // (mesh_rows * mesh_cols)
    row_span = GRID // mesh_rows
    col_span = GRID // mesh_cols
    steps = jnp.arange(GRID, dtype=jnp.int32)

    mirror = mesh_cols - 1 - col_pos
    low = jnp.minimum(col_pos, mirror)
    side = col_pos // (mesh_cols // 2)
    span_z = col_span + 1
    x_half = row_span // 2
    by_block = gmap.reshape(mesh_rows, mesh_cols, per_device)
    direct = lax.dynamic_index_in_dim(by_block, low, axis=1, keepdims=False)
    mirrored = lax.dynamic_index_in_dim(by_block, mesh_cols - 1 - low, axis=1, keepdims=False)
    both = jnp.stack([direct, mirrored], axis=1).reshape(-1)
    flip = (jnp.arange(both.shape[0], dtype=jnp.int32) // per_device) % 2
    freq_x = both // (GRID * GRID)
    freq_y = both // GRID % GRID
    freq_z = both % GRID
    freq_x = jnp.where(flip == 1, (GRID - freq_x) % GRID, freq_x)
    freq_y = jnp.where(flip == 1, (GRID - freq_y) % GRID, freq_y)
    freq_z = jnp.where(flip == 1, (GRID - freq_z) % GRID, freq_z) - low * col_span
    sign = jnp.where(flip == 1, -1.0, 1.0).astype(jnp.float32)
    pick = freq_y * span_z + freq_z
    x_glob = row_pos * row_span + side * x_half + jnp.arange(x_half, dtype=jnp.int32)
    cos_x, sin_x = phase_table(x_glob, freq_x, GRID)

    kz_set = (jnp.arange(mesh_cols // 2, dtype=jnp.int32)[:, None] * col_span
              + jnp.arange(span_z, dtype=jnp.int32)[None, :]).reshape(-1)
    cos_z, sin_z = phase_table(steps, kz_set, GRID)
    table_z = jnp.stack([cos_z, -sin_z], axis=-1).reshape(GRID, mesh_cols // 2, span_z, 2)
    table_z = jnp.stack([table_z, table_z[:, ::-1]], axis=0)
    cos_y, sin_y = phase_table(steps, steps, GRID)
    table_y = jnp.stack(
        [jnp.stack([cos_y, -sin_y], axis=-1), jnp.stack([sin_y, cos_y], axis=-1)], axis=1
    ).reshape(mesh_cols, col_span, 2, GRID, 2)

    sizes = [x_half // 4, x_half // 2, x_half // 4]
    pieces = []
    for i, chunk in enumerate(sizes):
        start = sum(sizes[:i])
        lo = slice(start, start + chunk)
        hi = slice(x_half + start, x_half + start + chunk)
        band_v = jnp.stack([psi_val[:, lo], psi_val[:, hi]], axis=1)
        band_c = jnp.stack([psi_cond[:, lo], psi_cond[:, hi]], axis=1)
        rho = jnp.take(band_v, val_index, axis=0, mode="clip") * jnp.take(
            band_c, cond_index, axis=0, mode="clip"
        )
        z_all = jnp.einsum("phxyz,hzcjt->hcpxyjt", rho, table_z, precision=HIGH)
        z_all = z_all.reshape((mesh_cols,) + z_all.shape[2:])
        z_mine = lax.all_to_all(z_all, "col", split_axis=0, concat_axis=0, tiled=True)
        if i >= 1:
            z_mine, pieces[i - 1] = lax.optimization_barrier((z_mine, pieces[i - 1]))
        y_all = jnp.einsum("spxyjt,syteu->ejuxp", z_mine, table_y, precision=HIGH)
        flat = y_all.reshape(GRID * span_z, 2 * chunk * pairs)
        chosen = jnp.take(flat, pick, axis=0, mode="clip").reshape(-1, 2, chunk, pairs)
        c_re = chosen[:, 0]
        c_im = chosen[:, 1]
        cx = cos_x[lo].T[:, :, None]
        sx = sin_x[lo].T[:, :, None]
        part_re = jnp.sum(c_re * cx + c_im * sx, axis=1)
        part_im = jnp.sum(c_im * cx - c_re * sx, axis=1)
        pieces.append(jnp.stack([part_re, part_im], axis=1))
    partial = pieces[0]
    for piece in pieces[1:]:
        partial = partial + piece
    partial = partial * jnp.stack([jnp.ones_like(sign), sign], axis=1)[:, :, None] * scale
    block = 2 * per_device
    spread = partial.reshape(mesh_rows, block, 2, pairs)
    gathered = lax.all_to_all(spread, "row", split_axis=0, concat_axis=0, tiled=True)
    both_blocks = jnp.sum(gathered, axis=0).reshape(2, per_device, 2, pairs)
    mine = lax.dynamic_index_in_dim(both_blocks, side, axis=0, keepdims=False)
    theirs = lax.dynamic_index_in_dim(both_blocks, 1 - side, axis=0, keepdims=False)
    partner = lax.ppermute(theirs, "col", [(c, mesh_cols - 1 - c) for c in range(mesh_cols)])
    own = mine + partner
    copies = jnp.broadcast_to(own[None], (mesh_cols,) + own.shape)
    row_blocks = lax.all_to_all(copies, "col", split_axis=0, concat_axis=0, tiled=True)
    rows = row_blocks.reshape(mesh_cols * per_device, 2, pairs)
    half = mesh_cols // 2
    send = lax.dynamic_slice_in_dim(rows, (col_pos // half) * half * per_device, half * per_device, 0)
    perm = []
    for src_r in range(mesh_rows):
        for src_c in range(mesh_cols):
            dst_r = src_c % half
            dst_c = 2 * src_r + src_c // half
            perm.append((src_r * mesh_cols + src_c, dst_r * mesh_cols + dst_c))
    cols = lax.ppermute(send, ("row", "col"), perm)

    val_hot = val_index[:, None] == jnp.arange(eps_val.shape[0], dtype=jnp.int32)[None, :]
    cond_hot = cond_index[:, None] == jnp.arange(eps_cond.shape[0], dtype=jnp.int32)[None, :]
    energy_v = jnp.sum(jnp.where(val_hot, eps_val[None, :], 0.0), axis=1)
    energy_c = jnp.sum(jnp.where(cond_hot, eps_cond[None, :], 0.0), axis=1)
    weight = (-6.0 / (math.sqrt(pairs) * (energy_c - energy_v)))[None, :]
    rows_re = rows[:, 0]
    rows_im = rows[:, 1]
    cols_re = cols[:, 0]
    cols_im = cols[:, 1]
    out_re = (
        chi0_in[0]
        + contract_pairs(weight * rows_re, cols_re)
        + contract_pairs(weight * rows_im, cols_im)
    )
    out_im = (
        chi0_in[1]
        + contract_pairs(weight * rows_im, cols_re)
        - contract_pairs(weight * rows_re, cols_im)
    )
    return jnp.stack([out_re, out_im])


def solution(mesh):
    return jax.shard_map(
        on_device,
        mesh=mesh,
        in_specs=(
            P(None, "row", "col", None),
            P(None, "row", "col", None),
            P(),
            P(),
            P(),
            P(),
            P(),
            P(None, "row", "col"),
        ),
        out_specs=P(None, "row", "col"),
        check_vma=False,
    )
```

```python
import math

import jax
import numpy as np
import jax.numpy as jnp
from jax import lax
from jax.sharding import PartitionSpec as P

GRID = 128
NG = 8192


HIGH = lax.Precision.HIGHEST


def phase_table(left, right, length):
    phase = left[:, None] * right[None, :] % length
    angle = phase.astype(jnp.float32) * (2.0 * math.pi / length)
    return (jnp.cos(angle), jnp.sin(angle))


def contract_pairs(left, right):
    return lax.dot_general(
        left, right, (((1,), (1,)), ((), ())), precision=HIGH, preferred_element_type=jnp.float32
    )


def on_device(psi_val, psi_cond, eps_val, eps_cond, val_index, cond_index, gmap, chi0_in):
    pairs = val_index.shape[0]
    scale = 1.0 / math.sqrt(GRID**3)
    row_pos = lax.axis_index("row")
    col_pos = lax.axis_index("col")
    mesh_cols = lax.axis_size("col")
    mesh_rows = lax.axis_size("row")
    per_device = NG // (mesh_rows * mesh_cols)
    row_span = GRID // mesh_rows
    col_span = GRID // mesh_cols
    steps = jnp.arange(GRID, dtype=jnp.int32)

    mirror = mesh_cols - 1 - col_pos
    low = jnp.minimum(col_pos, mirror)
    side = col_pos // (mesh_cols // 2)
    span_z = col_span + 1
    x_half = row_span // 2
    by_block = gmap.reshape(mesh_rows, mesh_cols, per_device)
    direct = lax.dynamic_index_in_dim(by_block, low, axis=1, keepdims=False)
    mirrored = lax.dynamic_index_in_dim(by_block, mesh_cols - 1 - low, axis=1, keepdims=False)
    both = jnp.stack([direct, mirrored], axis=1).reshape(-1)
    flip = (jnp.arange(both.shape[0], dtype=jnp.int32) // per_device) % 2
    freq_x = both // (GRID * GRID)
    freq_y = both // GRID % GRID
    freq_z = both % GRID
    freq_x = jnp.where(flip == 1, (GRID - freq_x) % GRID, freq_x)
    freq_y = jnp.where(flip == 1, (GRID - freq_y) % GRID, freq_y)
    freq_z = jnp.where(flip == 1, (GRID - freq_z) % GRID, freq_z) - low * col_span
    sign = jnp.where(flip == 1, -1.0, 1.0).astype(jnp.float32)
    pick = freq_y * span_z + freq_z
    x_glob = row_pos * row_span + side * x_half + jnp.arange(x_half, dtype=jnp.int32)
    cos_x, sin_x = phase_table(x_glob, freq_x, GRID)

    kz_set = (jnp.arange(mesh_cols // 2, dtype=jnp.int32)[:, None] * col_span
              + jnp.arange(span_z, dtype=jnp.int32)[None, :]).reshape(-1)
    cos_z, sin_z = phase_table(steps, kz_set, GRID)
    table_z = jnp.stack([cos_z, -sin_z], axis=-1).reshape(GRID, mesh_cols // 2, span_z, 2)
    table_z = jnp.stack([table_z, table_z[:, ::-1]], axis=0)
    cos_y, sin_y = phase_table(steps, steps, GRID)
    table_y = jnp.stack(
        [jnp.stack([cos_y, -sin_y], axis=-1), jnp.stack([sin_y, cos_y], axis=-1)], axis=1
    ).reshape(mesh_cols, col_span, 2, GRID, 2)

    sizes = [x_half // 4, x_half // 2, x_half // 4]
    pieces = []
    for i, chunk in enumerate(sizes):
        start = sum(sizes[:i])
        lo = slice(start, start + chunk)
        hi = slice(x_half + start, x_half + start + chunk)
        band_v = jnp.stack([psi_val[:, lo], psi_val[:, hi]], axis=1)
        band_c = jnp.stack([psi_cond[:, lo], psi_cond[:, hi]], axis=1)
        rho = jnp.take(band_v, val_index, axis=0, mode="clip") * jnp.take(
            band_c, cond_index, axis=0, mode="clip"
        )
        z_all = jnp.einsum("phxyz,hzcjt->hcpxyjt", rho, table_z, precision=HIGH)
        z_all = z_all.reshape((mesh_cols,) + z_all.shape[2:])
        z_mine = lax.all_to_all(z_all, "col", split_axis=0, concat_axis=0, tiled=True)
        if i >= 1:
            z_mine, pieces[i - 1] = lax.optimization_barrier((z_mine, pieces[i - 1]))
        y_all = jnp.einsum("spxyjt,syteu->ejuxp", z_mine, table_y, precision=HIGH)
        flat = y_all.reshape(GRID * span_z, 2, chunk, pairs)
        chosen = jnp.take(flat, pick, axis=0, mode="clip")
        c_re = chosen[:, 0]
        c_im = chosen[:, 1]
        cx = cos_x[lo].T[:, :, None]
        sx = sin_x[lo].T[:, :, None]
        part_re = jnp.sum(c_re * cx + c_im * sx, axis=1)
        part_im = jnp.sum(c_im * cx - c_re * sx, axis=1)
        pieces.append(jnp.stack([part_re, part_im], axis=1))
    partial = pieces[0]
    for piece in pieces[1:]:
        partial = partial + piece
    partial = partial * jnp.stack([jnp.ones_like(sign), sign], axis=1)[:, :, None] * scale
    block = 2 * per_device
    spread = partial.reshape(mesh_rows, block, 2, pairs)
    gathered = lax.all_to_all(spread, "row", split_axis=0, concat_axis=0, tiled=True)
    both_blocks = jnp.sum(gathered, axis=0).reshape(2, per_device, 2, pairs)
    mine = lax.dynamic_index_in_dim(both_blocks, side, axis=0, keepdims=False)
    theirs = lax.dynamic_index_in_dim(both_blocks, 1 - side, axis=0, keepdims=False)
    partner = lax.ppermute(theirs, "col", [(c, mesh_cols - 1 - c) for c in range(mesh_cols)])
    own = mine + partner
    copies = jnp.broadcast_to(own[None], (mesh_cols,) + own.shape)
    row_blocks = lax.all_to_all(copies, "col", split_axis=0, concat_axis=0, tiled=True)
    rows = row_blocks.reshape(mesh_cols * per_device, 2, pairs)
    half = mesh_cols // 2
    send = lax.dynamic_slice_in_dim(rows, (col_pos // half) * half * per_device, half * per_device, 0)
    perm = []
    for src_r in range(mesh_rows):
        for src_c in range(mesh_cols):
            dst_r = src_c % half
            dst_c = 2 * src_r + src_c // half
            perm.append((src_r * mesh_cols + src_c, dst_r * mesh_cols + dst_c))
    cols = lax.ppermute(send, ("row", "col"), perm)

    val_hot = val_index[:, None] == jnp.arange(eps_val.shape[0], dtype=jnp.int32)[None, :]
    cond_hot = cond_index[:, None] == jnp.arange(eps_cond.shape[0], dtype=jnp.int32)[None, :]
    energy_v = jnp.sum(jnp.where(val_hot, eps_val[None, :], 0.0), axis=1)
    energy_c = jnp.sum(jnp.where(cond_hot, eps_cond[None, :], 0.0), axis=1)
    weight = (-6.0 / (math.sqrt(pairs) * (energy_c - energy_v)))[None, :]
    rows_re = rows[:, 0]
    rows_im = rows[:, 1]
    cols_re = cols[:, 0]
    cols_im = cols[:, 1]
    out_re = (
        chi0_in[0]
        + contract_pairs(weight * rows_re, cols_re)
        + contract_pairs(weight * rows_im, cols_im)
    )
    out_im = (
        chi0_in[1]
        + contract_pairs(weight * rows_im, cols_re)
        - contract_pairs(weight * rows_re, cols_im)
    )
    return jnp.stack([out_re, out_im])


def solution(mesh):
    return jax.shard_map(
        on_device,
        mesh=mesh,
        in_specs=(
            P(None, "row", "col", None),
            P(None, "row", "col", None),
            P(),
            P(),
            P(),
            P(),
            P(),
            P(None, "row", "col"),
        ),
        out_specs=P(None, "row", "col"),
        check_vma=False,
    )
```

```python
import math

import jax
import numpy as np
import jax.numpy as jnp
from jax import lax
from jax.sharding import PartitionSpec as P

GRID = 128
NG = 8192


HIGH = lax.Precision.HIGHEST


def phase_table(left, right, length):
    phase = left[:, None] * right[None, :] % length
    angle = phase.astype(jnp.float32) * (2.0 * math.pi / length)
    return (jnp.cos(angle), jnp.sin(angle))


def contract_pairs(left, right):
    return lax.dot_general(
        left, right, (((1,), (1,)), ((), ())), precision=HIGH, preferred_element_type=jnp.float32
    )


def on_device(psi_val, psi_cond, eps_val, eps_cond, val_index, cond_index, gmap, chi0_in):
    pairs = val_index.shape[0]
    scale = 1.0 / math.sqrt(GRID**3)
    row_pos = lax.axis_index("row")
    col_pos = lax.axis_index("col")
    mesh_cols = lax.axis_size("col")
    mesh_rows = lax.axis_size("row")
    per_device = NG // (mesh_rows * mesh_cols)
    row_span = GRID // mesh_rows
    col_span = GRID // mesh_cols
    steps = jnp.arange(GRID, dtype=jnp.int32)

    mirror = mesh_cols - 1 - col_pos
    low = jnp.minimum(col_pos, mirror)
    side = col_pos // (mesh_cols // 2)
    span_z = col_span + 1
    x_half = row_span // 2
    by_block = gmap.reshape(mesh_rows, mesh_cols, per_device)
    direct = lax.dynamic_index_in_dim(by_block, low, axis=1, keepdims=False)
    mirrored = lax.dynamic_index_in_dim(by_block, mesh_cols - 1 - low, axis=1, keepdims=False)
    both = jnp.stack([direct, mirrored], axis=1).reshape(-1)
    flip = (jnp.arange(both.shape[0], dtype=jnp.int32) // per_device) % 2
    freq_x = both // (GRID * GRID)
    freq_y = both // GRID % GRID
    freq_z = both % GRID
    freq_x = jnp.where(flip == 1, (GRID - freq_x) % GRID, freq_x)
    freq_y = jnp.where(flip == 1, (GRID - freq_y) % GRID, freq_y)
    freq_z = jnp.where(flip == 1, (GRID - freq_z) % GRID, freq_z) - low * col_span
    sign = jnp.where(flip == 1, -1.0, 1.0).astype(jnp.float32)
    pick = freq_y * span_z + freq_z
    x_glob = row_pos * row_span + side * x_half + jnp.arange(x_half, dtype=jnp.int32)
    cos_x, sin_x = phase_table(x_glob, freq_x, GRID)

    kz_set = (jnp.arange(mesh_cols // 2, dtype=jnp.int32)[:, None] * col_span
              + jnp.arange(span_z, dtype=jnp.int32)[None, :]).reshape(-1)
    cos_z, sin_z = phase_table(steps, kz_set, GRID)
    table_z = jnp.stack([cos_z, -sin_z], axis=-1).reshape(GRID, mesh_cols // 2, span_z, 2)
    table_z = jnp.stack([table_z, table_z[:, ::-1]], axis=0)
    cos_y, sin_y = phase_table(steps, steps, GRID)
    table_y = jnp.stack(
        [jnp.stack([cos_y, -sin_y], axis=-1), jnp.stack([sin_y, cos_y], axis=-1)], axis=1
    ).reshape(mesh_cols, col_span, 2, GRID, 2)

    sizes = [x_half // 4, x_half // 2, x_half // 4]
    pieces = []
    for i, chunk in enumerate(sizes):
        start = sum(sizes[:i])
        lo = slice(start, start + chunk)
        hi = slice(x_half + start, x_half + start + chunk)
        band_v = jnp.stack([psi_val[:, lo], psi_val[:, hi]], axis=1)
        band_c = jnp.stack([psi_cond[:, lo], psi_cond[:, hi]], axis=1)
        rho = jnp.take(band_v, val_index, axis=0) * jnp.take(band_c, cond_index, axis=0)
        z_all = jnp.einsum("phxyz,hzcjt->hcpxyjt", rho, table_z, precision=HIGH)
        z_all = z_all.reshape((mesh_cols,) + z_all.shape[2:])
        z_mine = lax.all_to_all(z_all, "col", split_axis=0, concat_axis=0, tiled=True)
        if i >= 1:
            z_mine, pieces[i - 1] = lax.optimization_barrier((z_mine, pieces[i - 1]))
        y_all = jnp.einsum("spxyjt,syteu->ejuxp", z_mine, table_y, precision=HIGH)
        flat = y_all.reshape(GRID * span_z, 2, chunk, pairs)
        chosen = jnp.take(flat, pick, axis=0)
        c_re = chosen[:, 0]
        c_im = chosen[:, 1]
        cx = cos_x[lo].T[:, :, None]
        sx = sin_x[lo].T[:, :, None]
        part_re = jnp.sum(c_re * cx + c_im * sx, axis=1)
        part_im = jnp.sum(c_im * cx - c_re * sx, axis=1)
        pieces.append(jnp.stack([part_re, part_im], axis=1))
    partial = pieces[0]
    for piece in pieces[1:]:
        partial = partial + piece
    partial = partial * jnp.stack([jnp.ones_like(sign), sign], axis=1)[:, :, None] * scale
    block = 2 * per_device
    spread = partial.reshape(mesh_rows, block, 2, pairs)
    gathered = lax.all_to_all(spread, "row", split_axis=0, concat_axis=0, tiled=True)
    both_blocks = jnp.sum(gathered, axis=0).reshape(2, per_device, 2, pairs)
    copies = jnp.broadcast_to(both_blocks[None], (mesh_cols,) + both_blocks.shape)
    got = lax.all_to_all(copies, "col", split_axis=0, concat_axis=0, tiled=True)
    where = np.arange(mesh_cols)
    slot = (where >= mesh_cols // 2).astype(np.int32)
    rows = got[where, slot] + got[mesh_cols - 1 - where, slot]
    rows = rows.reshape(mesh_cols * per_device, 2, pairs)
    half = mesh_cols // 2
    send = lax.dynamic_slice_in_dim(rows, (col_pos // half) * half * per_device, half * per_device, 0)
    perm = []
    for src_r in range(mesh_rows):
        for src_c in range(mesh_cols):
            dst_r = src_c % half
            dst_c = 2 * src_r + src_c // half
            perm.append((src_r * mesh_cols + src_c, dst_r * mesh_cols + dst_c))
    cols = lax.ppermute(send, ("row", "col"), perm)

    val_hot = val_index[:, None] == jnp.arange(eps_val.shape[0], dtype=jnp.int32)[None, :]
    cond_hot = cond_index[:, None] == jnp.arange(eps_cond.shape[0], dtype=jnp.int32)[None, :]
    energy_v = jnp.sum(jnp.where(val_hot, eps_val[None, :], 0.0), axis=1)
    energy_c = jnp.sum(jnp.where(cond_hot, eps_cond[None, :], 0.0), axis=1)
    weight = (-6.0 / (math.sqrt(pairs) * (energy_c - energy_v)))[None, :]
    rows_re = rows[:, 0]
    rows_im = rows[:, 1]
    cols_re = cols[:, 0]
    cols_im = cols[:, 1]
    out_re = (
        chi0_in[0]
        + contract_pairs(weight * rows_re, cols_re)
        + contract_pairs(weight * rows_im, cols_im)
    )
    out_im = (
        chi0_in[1]
        + contract_pairs(weight * rows_im, cols_re)
        - contract_pairs(weight * rows_re, cols_im)
    )
    return jnp.stack([out_re, out_im])


def solution(mesh):
    return jax.shard_map(
        on_device,
        mesh=mesh,
        in_specs=(
            P(None, "row", "col", None),
            P(None, "row", "col", None),
            P(),
            P(),
            P(),
            P(),
            P(),
            P(None, "row", "col"),
        ),
        out_specs=P(None, "row", "col"),
        check_vma=False,
    )
```

```python
import math

import jax
import numpy as np
import jax.numpy as jnp
from jax import lax
from jax.sharding import PartitionSpec as P

GRID = 128
NG = 8192


HIGH = lax.Precision.HIGHEST
DFT = lax.Precision.HIGH


def phase_table(left, right, length):
    phase = left[:, None] * right[None, :] % length
    angle = phase.astype(jnp.float32) * (2.0 * math.pi / length)
    return (jnp.cos(angle), jnp.sin(angle))


def contract_pairs(left, right):
    return lax.dot_general(
        left, right, (((1,), (1,)), ((), ())), precision=HIGH, preferred_element_type=jnp.float32
    )


def on_device(psi_val, psi_cond, eps_val, eps_cond, val_index, cond_index, gmap, chi0_in):
    pairs = val_index.shape[0]
    scale = 1.0 / math.sqrt(GRID**3)
    row_pos = lax.axis_index("row")
    col_pos = lax.axis_index("col")
    mesh_cols = lax.axis_size("col")
    mesh_rows = lax.axis_size("row")
    per_device = NG // (mesh_rows * mesh_cols)
    row_span = GRID // mesh_rows
    col_span = GRID // mesh_cols
    steps = jnp.arange(GRID, dtype=jnp.int32)

    mirror = mesh_cols - 1 - col_pos
    low = jnp.minimum(col_pos, mirror)
    side = col_pos // (mesh_cols // 2)
    span_z = col_span + 1
    x_half = row_span // 2
    by_block = gmap.reshape(mesh_rows, mesh_cols, per_device)
    direct = lax.dynamic_index_in_dim(by_block, low, axis=1, keepdims=False)
    mirrored = lax.dynamic_index_in_dim(by_block, mesh_cols - 1 - low, axis=1, keepdims=False)
    both = jnp.stack([direct, mirrored], axis=1).reshape(-1)
    flip = (jnp.arange(both.shape[0], dtype=jnp.int32) // per_device) % 2
    freq_x = both // (GRID * GRID)
    freq_y = both // GRID % GRID
    freq_z = both % GRID
    freq_x = jnp.where(flip == 1, (GRID - freq_x) % GRID, freq_x)
    freq_y = jnp.where(flip == 1, (GRID - freq_y) % GRID, freq_y)
    freq_z = jnp.where(flip == 1, (GRID - freq_z) % GRID, freq_z) - low * col_span
    sign = jnp.where(flip == 1, -1.0, 1.0).astype(jnp.float32)
    pick = freq_y * span_z + freq_z
    x_glob = row_pos * row_span + side * x_half + jnp.arange(x_half, dtype=jnp.int32)
    cos_x, sin_x = phase_table(x_glob, freq_x, GRID)

    kz_set = (jnp.arange(mesh_cols // 2, dtype=jnp.int32)[:, None] * col_span
              + jnp.arange(span_z, dtype=jnp.int32)[None, :]).reshape(-1)
    cos_z, sin_z = phase_table(steps, kz_set, GRID)
    table_z = jnp.stack([cos_z, -sin_z], axis=-1).reshape(GRID, mesh_cols // 2, span_z, 2)
    table_z = jnp.stack([table_z, table_z[:, ::-1]], axis=0)
    cos_y, sin_y = phase_table(steps, steps, GRID)
    table_y = jnp.stack(
        [jnp.stack([cos_y, -sin_y], axis=-1), jnp.stack([sin_y, cos_y], axis=-1)], axis=1
    ).reshape(mesh_cols, col_span, 2, GRID, 2)

    sizes = [x_half // 4, x_half // 2, x_half // 4]
    pieces = []
    for i, chunk in enumerate(sizes):
        start = sum(sizes[:i])
        lo = slice(start, start + chunk)
        hi = slice(x_half + start, x_half + start + chunk)
        band_v = jnp.stack([psi_val[:, lo], psi_val[:, hi]], axis=1)
        band_c = jnp.stack([psi_cond[:, lo], psi_cond[:, hi]], axis=1)
        rho = jnp.take(band_v, val_index, axis=0) * jnp.take(band_c, cond_index, axis=0)
        z_all = jnp.einsum("phxyz,hzcjt->hcpxyjt", rho, table_z, precision=DFT)
        z_all = z_all.reshape((mesh_cols,) + z_all.shape[2:])
        z_mine = lax.all_to_all(z_all, "col", split_axis=0, concat_axis=0, tiled=True)
        if i >= 1:
            z_mine, pieces[i - 1] = lax.optimization_barrier((z_mine, pieces[i - 1]))
        y_all = jnp.einsum("spxyjt,syteu->ejuxp", z_mine, table_y, precision=DFT)
        flat = y_all.reshape(GRID * span_z, 2, chunk, pairs)
        chosen = jnp.take(flat, pick, axis=0)
        c_re = chosen[:, 0]
        c_im = chosen[:, 1]
        cx = cos_x[lo].T[:, :, None]
        sx = sin_x[lo].T[:, :, None]
        part_re = jnp.sum(c_re * cx + c_im * sx, axis=1)
        part_im = jnp.sum(c_im * cx - c_re * sx, axis=1)
        pieces.append(jnp.stack([part_re, part_im], axis=1))
    partial = pieces[0]
    for piece in pieces[1:]:
        partial = partial + piece
    partial = partial * jnp.stack([jnp.ones_like(sign), sign], axis=1)[:, :, None] * scale
    block = 2 * per_device
    spread = partial.reshape(mesh_rows, block, 2, pairs)
    gathered = lax.all_to_all(spread, "row", split_axis=0, concat_axis=0, tiled=True)
    both_blocks = jnp.sum(gathered, axis=0).reshape(2, per_device, 2, pairs)
    mine = lax.dynamic_index_in_dim(both_blocks, side, axis=0, keepdims=False)
    theirs = lax.dynamic_index_in_dim(both_blocks, 1 - side, axis=0, keepdims=False)
    partner = lax.ppermute(theirs, "col", [(c, mesh_cols - 1 - c) for c in range(mesh_cols)])
    own = mine + partner
    copies = jnp.broadcast_to(own[None], (mesh_cols,) + own.shape)
    row_blocks = lax.all_to_all(copies, "col", split_axis=0, concat_axis=0, tiled=True)
    rows = row_blocks.reshape(mesh_cols * per_device, 2, pairs)
    half = mesh_cols // 2
    send = lax.dynamic_slice_in_dim(rows, (col_pos // half) * half * per_device, half * per_device, 0)
    perm = []
    for src_r in range(mesh_rows):
        for src_c in range(mesh_cols):
            dst_r = src_c % half
            dst_c = 2 * src_r + src_c // half
            perm.append((src_r * mesh_cols + src_c, dst_r * mesh_cols + dst_c))
    cols = lax.ppermute(send, ("row", "col"), perm)

    val_hot = val_index[:, None] == jnp.arange(eps_val.shape[0], dtype=jnp.int32)[None, :]
    cond_hot = cond_index[:, None] == jnp.arange(eps_cond.shape[0], dtype=jnp.int32)[None, :]
    energy_v = jnp.sum(jnp.where(val_hot, eps_val[None, :], 0.0), axis=1)
    energy_c = jnp.sum(jnp.where(cond_hot, eps_cond[None, :], 0.0), axis=1)
    weight = (-6.0 / (math.sqrt(pairs) * (energy_c - energy_v)))[None, :]
    rows_re = rows[:, 0]
    rows_im = rows[:, 1]
    cols_re = cols[:, 0]
    cols_im = cols[:, 1]
    out_re = (
        chi0_in[0]
        + contract_pairs(weight * rows_re, cols_re)
        + contract_pairs(weight * rows_im, cols_im)
    )
    out_im = (
        chi0_in[1]
        + contract_pairs(weight * rows_im, cols_re)
        - contract_pairs(weight * rows_re, cols_im)
    )
    return jnp.stack([out_re, out_im])


def solution(mesh):
    return jax.shard_map(
        on_device,
        mesh=mesh,
        in_specs=(
            P(None, "row", "col", None),
            P(None, "row", "col", None),
            P(),
            P(),
            P(),
            P(),
            P(),
            P(None, "row", "col"),
        ),
        out_specs=P(None, "row", "col"),
        check_vma=False,
    )
```

```python
import math

import jax
import numpy as np
import jax.numpy as jnp
from jax import lax
from jax.sharding import PartitionSpec as P

GRID = 128
NG = 8192


HIGH = lax.Precision.HIGHEST


def phase_table(left, right, length):
    phase = left[:, None] * right[None, :] % length
    angle = phase.astype(jnp.float32) * (2.0 * math.pi / length)
    return (jnp.cos(angle), jnp.sin(angle))


def contract_pairs(left, right):
    return lax.dot_general(
        left, right, (((1,), (1,)), ((), ())), precision=HIGH, preferred_element_type=jnp.float32
    )


def on_device(psi_val, psi_cond, eps_val, eps_cond, val_index, cond_index, gmap, chi0_in):
    pairs = val_index.shape[0]
    scale = 1.0 / math.sqrt(GRID**3)
    row_pos = lax.axis_index("row")
    col_pos = lax.axis_index("col")
    mesh_cols = lax.axis_size("col")
    mesh_rows = lax.axis_size("row")
    per_device = NG // (mesh_rows * mesh_cols)
    row_span = GRID // mesh_rows
    col_span = GRID // mesh_cols
    steps = jnp.arange(GRID, dtype=jnp.int32)

    mirror = mesh_cols - 1 - col_pos
    low = jnp.minimum(col_pos, mirror)
    side = col_pos // (mesh_cols // 2)
    span_z = col_span + 1
    x_half = row_span // 2
    by_block = gmap.reshape(mesh_rows, mesh_cols, per_device)
    direct = lax.dynamic_index_in_dim(by_block, low, axis=1, keepdims=False)
    mirrored = lax.dynamic_index_in_dim(by_block, mesh_cols - 1 - low, axis=1, keepdims=False)
    both = jnp.stack([direct, mirrored], axis=1).reshape(-1)
    flip = (jnp.arange(both.shape[0], dtype=jnp.int32) // per_device) % 2
    freq_x = both // (GRID * GRID)
    freq_y = both // GRID % GRID
    freq_z = both % GRID
    freq_x = jnp.where(flip == 1, (GRID - freq_x) % GRID, freq_x)
    freq_y = jnp.where(flip == 1, (GRID - freq_y) % GRID, freq_y)
    freq_z = jnp.where(flip == 1, (GRID - freq_z) % GRID, freq_z) - low * col_span
    sign = jnp.where(flip == 1, -1.0, 1.0).astype(jnp.float32)
    pick = freq_y * span_z + freq_z
    x_glob = row_pos * row_span + side * x_half + jnp.arange(x_half, dtype=jnp.int32)
    cos_x, sin_x = phase_table(x_glob, freq_x, GRID)

    kz_set = (jnp.arange(mesh_cols // 2, dtype=jnp.int32)[:, None] * col_span
              + jnp.arange(span_z, dtype=jnp.int32)[None, :]).reshape(-1)
    cos_z, sin_z = phase_table(steps, kz_set, GRID)
    table_z = jnp.stack([cos_z, -sin_z], axis=-1).reshape(GRID, mesh_cols // 2, span_z, 2)
    table_z = jnp.stack([table_z, table_z[:, ::-1]], axis=0)
    cos_y, sin_y = phase_table(steps, steps, GRID)
    table_y = jnp.stack(
        [jnp.stack([cos_y, -sin_y], axis=-1), jnp.stack([sin_y, cos_y], axis=-1)], axis=1
    ).reshape(mesh_cols, col_span, 2, GRID, 2)

    sizes = [x_half // 4, x_half // 2, x_half // 4]
    pieces = []
    for i, chunk in enumerate(sizes):
        start = sum(sizes[:i])
        lo = slice(start, start + chunk)
        hi = slice(x_half + start, x_half + start + chunk)
        band_v = jnp.stack([psi_val[:, lo], psi_val[:, hi]], axis=1)
        band_c = jnp.stack([psi_cond[:, lo], psi_cond[:, hi]], axis=1)
        if i >= 1:
            band_v, band_c, z_all = lax.optimization_barrier((band_v, band_c, z_all))
        rho = jnp.take(band_v, val_index, axis=0) * jnp.take(band_c, cond_index, axis=0)
        z_all = jnp.einsum("phxyz,hzcjt->hcpxyjt", rho, table_z, precision=HIGH)
        z_all = z_all.reshape((mesh_cols,) + z_all.shape[2:])
        z_mine = lax.all_to_all(z_all, "col", split_axis=0, concat_axis=0, tiled=True)
        if i >= 1:
            z_mine, pieces[i - 1] = lax.optimization_barrier((z_mine, pieces[i - 1]))
        y_all = jnp.einsum("spxyjt,syteu->ejuxp", z_mine, table_y, precision=HIGH)
        flat = y_all.reshape(GRID * span_z, 2, chunk, pairs)
        chosen = jnp.take(flat, pick, axis=0)
        c_re = chosen[:, 0]
        c_im = chosen[:, 1]
        cx = cos_x[lo].T[:, :, None]
        sx = sin_x[lo].T[:, :, None]
        part_re = jnp.sum(c_re * cx + c_im * sx, axis=1)
        part_im = jnp.sum(c_im * cx - c_re * sx, axis=1)
        pieces.append(jnp.stack([part_re, part_im], axis=1))
    partial = pieces[0]
    for piece in pieces[1:]:
        partial = partial + piece
    partial = partial * jnp.stack([jnp.ones_like(sign), sign], axis=1)[:, :, None] * scale
    block = 2 * per_device
    spread = partial.reshape(mesh_rows, block, 2, pairs)
    gathered = lax.all_to_all(spread, "row", split_axis=0, concat_axis=0, tiled=True)
    both_blocks = jnp.sum(gathered, axis=0).reshape(2, per_device, 2, pairs)
    mine = lax.dynamic_index_in_dim(both_blocks, side, axis=0, keepdims=False)
    theirs = lax.dynamic_index_in_dim(both_blocks, 1 - side, axis=0, keepdims=False)
    partner = lax.ppermute(theirs, "col", [(c, mesh_cols - 1 - c) for c in range(mesh_cols)])
    own = mine + partner
    copies = jnp.broadcast_to(own[None], (mesh_cols,) + own.shape)
    row_blocks = lax.all_to_all(copies, "col", split_axis=0, concat_axis=0, tiled=True)
    rows = row_blocks.reshape(mesh_cols * per_device, 2, pairs)
    half = mesh_cols // 2
    send = lax.dynamic_slice_in_dim(rows, (col_pos // half) * half * per_device, half * per_device, 0)
    perm = []
    for src_r in range(mesh_rows):
        for src_c in range(mesh_cols):
            dst_r = src_c % half
            dst_c = 2 * src_r + src_c // half
            perm.append((src_r * mesh_cols + src_c, dst_r * mesh_cols + dst_c))
    cols = lax.ppermute(send, ("row", "col"), perm)

    val_hot = val_index[:, None] == jnp.arange(eps_val.shape[0], dtype=jnp.int32)[None, :]
    cond_hot = cond_index[:, None] == jnp.arange(eps_cond.shape[0], dtype=jnp.int32)[None, :]
    energy_v = jnp.sum(jnp.where(val_hot, eps_val[None, :], 0.0), axis=1)
    energy_c = jnp.sum(jnp.where(cond_hot, eps_cond[None, :], 0.0), axis=1)
    weight = (-6.0 / (math.sqrt(pairs) * (energy_c - energy_v)))[None, :]
    rows_re = rows[:, 0]
    rows_im = rows[:, 1]
    cols_re = cols[:, 0]
    cols_im = cols[:, 1]
    out_re = (
        chi0_in[0]
        + contract_pairs(weight * rows_re, cols_re)
        + contract_pairs(weight * rows_im, cols_im)
    )
    out_im = (
        chi0_in[1]
        + contract_pairs(weight * rows_im, cols_re)
        - contract_pairs(weight * rows_re, cols_im)
    )
    return jnp.stack([out_re, out_im])


def solution(mesh):
    return jax.shard_map(
        on_device,
        mesh=mesh,
        in_specs=(
            P(None, "row", "col", None),
            P(None, "row", "col", None),
            P(),
            P(),
            P(),
            P(),
            P(),
            P(None, "row", "col"),
        ),
        out_specs=P(None, "row", "col"),
        check_vma=False,
    )
```

```python
import math

import jax
import numpy as np
import jax.numpy as jnp
from jax import lax
from jax.sharding import PartitionSpec as P

GRID = 128
NG = 8192


HIGH = lax.Precision.HIGHEST


def phase_table(left, right, length):
    phase = left[:, None] * right[None, :] % length
    angle = phase.astype(jnp.float32) * (2.0 * math.pi / length)
    return (jnp.cos(angle), jnp.sin(angle))


def contract_pairs(left, right):
    return lax.dot_general(
        left, right, (((1,), (1,)), ((), ())), precision=HIGH, preferred_element_type=jnp.float32
    )


def on_device(psi_val, psi_cond, eps_val, eps_cond, val_index, cond_index, gmap, chi0_in):
    pairs = val_index.shape[0]
    scale = 1.0 / math.sqrt(GRID**3)
    row_pos = lax.axis_index("row")
    col_pos = lax.axis_index("col")
    mesh_cols = lax.axis_size("col")
    mesh_rows = lax.axis_size("row")
    per_device = NG // (mesh_rows * mesh_cols)
    row_span = GRID // mesh_rows
    col_span = GRID // mesh_cols
    steps = jnp.arange(GRID, dtype=jnp.int32)

    mirror = mesh_cols - 1 - col_pos
    low = jnp.minimum(col_pos, mirror)
    side = col_pos // (mesh_cols // 2)
    span_z = col_span + 1
    x_half = row_span // 2
    by_block = gmap.reshape(mesh_rows, mesh_cols, per_device)
    direct = lax.dynamic_index_in_dim(by_block, low, axis=1, keepdims=False)
    mirrored = lax.dynamic_index_in_dim(by_block, mesh_cols - 1 - low, axis=1, keepdims=False)
    both = jnp.stack([direct, mirrored], axis=1).reshape(-1)
    flip = (jnp.arange(both.shape[0], dtype=jnp.int32) // per_device) % 2
    freq_x = both // (GRID * GRID)
    freq_y = both // GRID % GRID
    freq_z = both % GRID
    freq_x = jnp.where(flip == 1, (GRID - freq_x) % GRID, freq_x)
    freq_y = jnp.where(flip == 1, (GRID - freq_y) % GRID, freq_y)
    freq_z = jnp.where(flip == 1, (GRID - freq_z) % GRID, freq_z) - low * col_span
    sign = jnp.where(flip == 1, -1.0, 1.0).astype(jnp.float32)
    pick = freq_y * span_z + freq_z
    x_glob = row_pos * row_span + side * x_half + jnp.arange(x_half, dtype=jnp.int32)
    cos_x, sin_x = phase_table(x_glob, freq_x, GRID)

    kz_set = (jnp.arange(mesh_cols // 2, dtype=jnp.int32)[:, None] * col_span
              + jnp.arange(span_z, dtype=jnp.int32)[None, :]).reshape(-1)
    cos_z, sin_z = phase_table(steps, kz_set, GRID)
    table_z = jnp.stack([cos_z, -sin_z], axis=-1).reshape(GRID, mesh_cols // 2, span_z, 2)
    table_z = jnp.stack([table_z, table_z[:, ::-1]], axis=0)
    cos_y, sin_y = phase_table(steps, steps, GRID)
    table_y = jnp.stack(
        [jnp.stack([cos_y, -sin_y], axis=-1), jnp.stack([sin_y, cos_y], axis=-1)], axis=1
    ).reshape(mesh_cols, col_span, 2, GRID, 2)

    sizes = [x_half // 4, x_half // 2, x_half // 4]
    pieces = []
    for i, chunk in enumerate(sizes):
        start = sum(sizes[:i])
        lo = slice(start, start + chunk)
        hi = slice(x_half + start, x_half + start + chunk)
        band_v = jnp.stack([psi_val[:, lo], psi_val[:, hi]], axis=1)
        band_c = jnp.stack([psi_cond[:, lo], psi_cond[:, hi]], axis=1)
        if i >= 1:
            band_v, band_c, z_all = lax.optimization_barrier((band_v, band_c, z_all))
        rho = jnp.take(band_v, val_index, axis=0, mode="clip") * jnp.take(
            band_c, cond_index, axis=0, mode="clip"
        )
        z_all = jnp.einsum("phxyz,hzcjt->hcpxyjt", rho, table_z, precision=HIGH)
        z_all = z_all.reshape((mesh_cols,) + z_all.shape[2:])
        z_mine = lax.all_to_all(z_all, "col", split_axis=0, concat_axis=0, tiled=True)
        if i >= 1:
            z_mine, pieces[i - 1] = lax.optimization_barrier((z_mine, pieces[i - 1]))
        y_all = jnp.einsum("spxyjt,syteu->ejuxp", z_mine, table_y, precision=HIGH)
        flat = y_all.reshape(GRID * span_z, 2, chunk, pairs)
        chosen = jnp.take(flat, pick, axis=0)
        c_re = chosen[:, 0]
        c_im = chosen[:, 1]
        cx = cos_x[lo].T[:, :, None]
        sx = sin_x[lo].T[:, :, None]
        part_re = jnp.sum(c_re * cx + c_im * sx, axis=1)
        part_im = jnp.sum(c_im * cx - c_re * sx, axis=1)
        pieces.append(jnp.stack([part_re, part_im], axis=1))
    partial = pieces[0]
    for piece in pieces[1:]:
        partial = partial + piece
    partial = partial * jnp.stack([jnp.ones_like(sign), sign], axis=1)[:, :, None] * scale
    block = 2 * per_device
    spread = partial.reshape(mesh_rows, block, 2, pairs)
    gathered = lax.all_to_all(spread, "row", split_axis=0, concat_axis=0, tiled=True)
    both_blocks = jnp.sum(gathered, axis=0).reshape(2, per_device, 2, pairs)
    mine = lax.dynamic_index_in_dim(both_blocks, side, axis=0, keepdims=False)
    theirs = lax.dynamic_index_in_dim(both_blocks, 1 - side, axis=0, keepdims=False)
    partner = lax.ppermute(theirs, "col", [(c, mesh_cols - 1 - c) for c in range(mesh_cols)])
    own = mine + partner
    copies = jnp.broadcast_to(own[None], (mesh_cols,) + own.shape)
    row_blocks = lax.all_to_all(copies, "col", split_axis=0, concat_axis=0, tiled=True)
    rows = row_blocks.reshape(mesh_cols * per_device, 2, pairs)
    half = mesh_cols // 2
    send = lax.dynamic_slice_in_dim(rows, (col_pos // half) * half * per_device, half * per_device, 0)
    perm = []
    for src_r in range(mesh_rows):
        for src_c in range(mesh_cols):
            dst_r = src_c % half
            dst_c = 2 * src_r + src_c // half
            perm.append((src_r * mesh_cols + src_c, dst_r * mesh_cols + dst_c))
    cols = lax.ppermute(send, ("row", "col"), perm)

    val_hot = val_index[:, None] == jnp.arange(eps_val.shape[0], dtype=jnp.int32)[None, :]
    cond_hot = cond_index[:, None] == jnp.arange(eps_cond.shape[0], dtype=jnp.int32)[None, :]
    energy_v = jnp.sum(jnp.where(val_hot, eps_val[None, :], 0.0), axis=1)
    energy_c = jnp.sum(jnp.where(cond_hot, eps_cond[None, :], 0.0), axis=1)
    weight = (-6.0 / (math.sqrt(pairs) * (energy_c - energy_v)))[None, :]
    rows_re = rows[:, 0]
    rows_im = rows[:, 1]
    cols_re = cols[:, 0]
    cols_im = cols[:, 1]
    out_re = (
        chi0_in[0]
        + contract_pairs(weight * rows_re, cols_re)
        + contract_pairs(weight * rows_im, cols_im)
    )
    out_im = (
        chi0_in[1]
        + contract_pairs(weight * rows_im, cols_re)
        - contract_pairs(weight * rows_re, cols_im)
    )
    return jnp.stack([out_re, out_im])


def solution(mesh):
    return jax.shard_map(
        on_device,
        mesh=mesh,
        in_specs=(
            P(None, "row", "col", None),
            P(None, "row", "col", None),
            P(),
            P(),
            P(),
            P(),
            P(),
            P(None, "row", "col"),
        ),
        out_specs=P(None, "row", "col"),
        check_vma=False,
    )
```

```python
import math

import jax
import numpy as np
import jax.numpy as jnp
from jax import lax
from jax.sharding import PartitionSpec as P

GRID = 128
NG = 8192


HIGH = lax.Precision.HIGHEST


def phase_table(left, right, length):
    phase = left[:, None] * right[None, :] % length
    angle = phase.astype(jnp.float32) * (2.0 * math.pi / length)
    return (jnp.cos(angle), jnp.sin(angle))


def contract_pairs(left, right):
    return lax.dot_general(
        left, right, (((1,), (1,)), ((), ())), precision=HIGH, preferred_element_type=jnp.float32
    )


def on_device(psi_val, psi_cond, eps_val, eps_cond, val_index, cond_index, gmap, chi0_in):
    pairs = val_index.shape[0]
    scale = 1.0 / math.sqrt(GRID**3)
    row_pos = lax.axis_index("row")
    col_pos = lax.axis_index("col")
    mesh_cols = lax.axis_size("col")
    mesh_rows = lax.axis_size("row")
    per_device = NG // (mesh_rows * mesh_cols)
    row_span = GRID // mesh_rows
    col_span = GRID // mesh_cols
    steps = jnp.arange(GRID, dtype=jnp.int32)

    mirror = mesh_cols - 1 - col_pos
    low = jnp.minimum(col_pos, mirror)
    side = col_pos // (mesh_cols // 2)
    span_z = col_span + 1
    x_half = row_span // 2
    by_block = gmap.reshape(mesh_rows, mesh_cols, per_device)
    direct = lax.dynamic_index_in_dim(by_block, low, axis=1, keepdims=False)
    mirrored = lax.dynamic_index_in_dim(by_block, mesh_cols - 1 - low, axis=1, keepdims=False)
    both = jnp.stack([direct, mirrored], axis=1).reshape(-1)
    flip = (jnp.arange(both.shape[0], dtype=jnp.int32) // per_device) % 2
    freq_x = both // (GRID * GRID)
    freq_y = both // GRID % GRID
    freq_z = both % GRID
    freq_x = jnp.where(flip == 1, (GRID - freq_x) % GRID, freq_x)
    freq_y = jnp.where(flip == 1, (GRID - freq_y) % GRID, freq_y)
    freq_z = jnp.where(flip == 1, (GRID - freq_z) % GRID, freq_z) - low * col_span
    sign = jnp.where(flip == 1, -1.0, 1.0).astype(jnp.float32)
    pick = freq_y * span_z + freq_z
    x_glob = row_pos * row_span + side * x_half + jnp.arange(x_half, dtype=jnp.int32)
    cos_x, sin_x = phase_table(x_glob, freq_x, GRID)

    kz_set = (jnp.arange(mesh_cols // 2, dtype=jnp.int32)[:, None] * col_span
              + jnp.arange(span_z, dtype=jnp.int32)[None, :]).reshape(-1)
    cos_z, sin_z = phase_table(steps, kz_set, GRID)
    table_z = jnp.stack([cos_z, -sin_z], axis=-1).reshape(GRID, mesh_cols // 2, span_z, 2)
    table_z = jnp.stack([table_z, table_z[:, ::-1]], axis=0)
    cos_y, sin_y = phase_table(steps, steps, GRID)
    table_y = jnp.stack(
        [jnp.stack([cos_y, -sin_y], axis=-1), jnp.stack([sin_y, cos_y], axis=-1)], axis=1
    ).reshape(mesh_cols, col_span, 2, GRID, 2)

    sizes = [x_half // 4, x_half // 2, x_half // 4]
    pieces = []
    for i, chunk in enumerate(sizes):
        start = sum(sizes[:i])
        lo = slice(start, start + chunk)
        hi = slice(x_half + start, x_half + start + chunk)
        band_v = jnp.stack([psi_val[:, lo], psi_val[:, hi]], axis=1)
        band_c = jnp.stack([psi_cond[:, lo], psi_cond[:, hi]], axis=1)
        if i >= 1:
            band_v, band_c, z_all = lax.optimization_barrier((band_v, band_c, z_all))
        rho = jnp.take(band_v, val_index, axis=0, mode="clip") * jnp.take(
            band_c, cond_index, axis=0, mode="clip"
        )
        z_all = jnp.einsum("phxyz,hzcjt->hcpxyjt", rho, table_z, precision=HIGH)
        z_all = z_all.reshape((mesh_cols,) + z_all.shape[2:])
        z_mine = lax.all_to_all(z_all, "col", split_axis=0, concat_axis=0, tiled=True)
        if i >= 1:
            z_mine, pieces[i - 1] = lax.optimization_barrier((z_mine, pieces[i - 1]))
        y_all = jnp.einsum("spxyjt,syteu->ejuxp", z_mine, table_y, precision=HIGH)
        flat = y_all.reshape(GRID * span_z, 2, chunk, pairs)
        chosen = jnp.take(flat, pick, axis=0)
        c_re = chosen[:, 0]
        c_im = chosen[:, 1]
        cx = cos_x[lo].T[:, :, None]
        sx = sin_x[lo].T[:, :, None]
        part_re = jnp.sum(c_re * cx + c_im * sx, axis=1)
        part_im = jnp.sum(c_im * cx - c_re * sx, axis=1)
        pieces.append(jnp.stack([part_re, part_im], axis=1))
    partial = pieces[0]
    for piece in pieces[1:]:
        partial = partial + piece
    partial = partial * jnp.stack([jnp.ones_like(sign), sign], axis=1)[:, :, None] * scale
    block = 2 * per_device
    spread = partial.reshape(mesh_rows, block, 2, pairs)
    gathered = lax.all_to_all(spread, "row", split_axis=0, concat_axis=0, tiled=True)
    both_blocks = jnp.sum(gathered, axis=0).reshape(2, per_device, 2, pairs)
    mine = lax.dynamic_index_in_dim(both_blocks, side, axis=0, keepdims=False)
    theirs = lax.dynamic_index_in_dim(both_blocks, 1 - side, axis=0, keepdims=False)
    partner = lax.ppermute(theirs, "col", [(c, mesh_cols - 1 - c) for c in range(mesh_cols)])
    own = mine + partner
    copies = jnp.broadcast_to(own[None], (mesh_cols,) + own.shape)
    row_blocks = lax.all_to_all(copies, "col", split_axis=0, concat_axis=0, tiled=True)
    rows = row_blocks.reshape(mesh_cols * per_device, 2, pairs)
    half = mesh_cols // 2
    send = lax.dynamic_slice_in_dim(rows, (col_pos // half) * half * per_device, half * per_device, 0)
    perm = []
    for src_r in range(mesh_rows):
        for src_c in range(mesh_cols):
            dst_r = src_c % half
            dst_c = 2 * src_r + src_c // half
            perm.append((src_r * mesh_cols + src_c, dst_r * mesh_cols + dst_c))
    cols = lax.ppermute(send, ("row", "col"), perm)

    val_hot = val_index[:, None] == jnp.arange(eps_val.shape[0], dtype=jnp.int32)[None, :]
    cond_hot = cond_index[:, None] == jnp.arange(eps_cond.shape[0], dtype=jnp.int32)[None, :]
    energy_v = jnp.sum(jnp.where(val_hot, eps_val[None, :], 0.0), axis=1)
    energy_c = jnp.sum(jnp.where(cond_hot, eps_cond[None, :], 0.0), axis=1)
    weight = (-6.0 / (math.sqrt(pairs) * (energy_c - energy_v)))[None, :]
    left = jnp.concatenate([weight * rows[:, 0], weight * rows[:, 1]], axis=1)
    right_re = jnp.concatenate([cols[:, 0], cols[:, 1]], axis=1)
    right_im = jnp.concatenate([-cols[:, 1], cols[:, 0]], axis=1)
    out_re = chi0_in[0] + contract_pairs(left, right_re)
    out_im = chi0_in[1] + contract_pairs(left, right_im)
    return jnp.stack([out_re, out_im])


def solution(mesh):
    return jax.shard_map(
        on_device,
        mesh=mesh,
        in_specs=(
            P(None, "row", "col", None),
            P(None, "row", "col", None),
            P(),
            P(),
            P(),
            P(),
            P(),
            P(None, "row", "col"),
        ),
        out_specs=P(None, "row", "col"),
        check_vma=False,
    )
```
